128 devices in a mesh: mass: 4 (over x), tile: 32 (over z, y, core).
Axes of the slice: x: 4, y: 4, z: 4, core: 2. Of those that a mesh axis runs over, the one named last changes fastest.
Arguments:
- spectra: bfloat16 [12288, 4096], P(('mass', 'tile')), may hold values from -6 to 6
- window: int32 [12288, 1], P(('mass', 'tile')), may hold values from 0 to 3; in each aligned block of 96 rows (0 to 95, 96 to 191, ...) at most 48 rows name the same one
- cluster: int32 [12288], P(('mass', 'tile')), may hold values from 0 to 127
Outputs:
- gram_tiles: float32 [24576, 6144], P(('mass', 'tile'))
- consensus: float32 [512, 4096], P(('mass', 'tile'))
The draws below stay inside these ranges and needn't reach their ends.
Inputs may be any that keep to these rules, and one draw needn't show every extreme that they name: Among the 96 spectra of one run shard, at most 48 name one window, and in every draw some window is named by exactly 48 of some shard.
All inputs are finite; a program needn't handle non-finite values.
Results may differ from the reference program's by a relative error of at most 0.0029.
Values may be sent and summed in bfloat16 or wider, within the bound.
No kernel may reach another device: no remote copies, remote signals or barrier semaphores. Data moves between devices by JAX's collectives and lax.ppermute only.
A program may use at most 192 MiB of HBM per device.

```python
import math
import jax
import jax.numpy as jnp
import numpy as np
from jax import lax

BINS = 4096
S_DEV = 96
SPECTRA = 12288
CAP = 48
SLOTS = 192
GROUP = 6144
CL_WIN = 128
CLUSTERS = 512
N_MASS = 4
N_TILE = 32


def place_ends(entries, rng, low, largest):
    place = [jax.random.randint(jax.random.fold_in(rng, axis), (), 0, length) for axis, length in enumerate(entries.shape)]
    main_axis = entries.shape.index(max(entries.shape))
    neighbour = place[:main_axis] + [(place[main_axis] + 1) % entries.shape[main_axis]] + place[main_axis + 1:]
    return entries.at[tuple(place)].set(low).at[tuple(neighbour)].set(largest)


def shard_levels(rng, extent, shards, low, top_value):
    level, own = 1.0, jax.random.fold_in(rng, 6)
    for position, parts in shards:
        steps = jnp.exp(jax.random.uniform(jax.random.fold_in(own, position), (parts,), jnp.float32, low / len(shards), top_value / len(shards)))
        level = level * jnp.repeat(steps, extent[position] // parts).reshape([-1 if axis == position else 1 for axis in range(len(extent))])
    return level


def assign_block(stream_key, own, number, rows, number_of, top, reach, skew):
    order = jax.random.permutation(stream_key, number_of)
    heavy_load, usual = portions_of(number_of, rows * top, reach, skew, True), portions_of(number_of, rows * top, reach, skew, False)
    places = jnp.arange(number_of)

    def named(lengths, turn):
        used = int((lengths > 0).sum())
        fixed = max(1, used // 4)
        shifted = fixed + (places - fixed + turn * (used - fixed)) % max(1, number_of - fixed)
        return jnp.zeros((number_of,), jnp.int32).at[order[jnp.where(places < fixed, places, shifted)]].set(jnp.asarray(lengths, jnp.int32))

    lengths = jnp.where(number % 4 == 0, named(heavy_load, number // 4), named(usual, number - number // 4 - 1))
    mixed = jax.random.permutation(jax.random.fold_in(own, 3), number_of)
    source_of, sink = mixed[0:number_of // 2 * 2:2], mixed[1:number_of // 2 * 2:2]
    slack = jnp.minimum(lengths[source_of] - 1, reach - lengths[sink]) // 2
    slack = jnp.where((source_of == order[0]) | (sink == order[0]) | (lengths[sink] == 0), 0, jnp.maximum(slack, 0))
    shifted = jax.random.randint(jax.random.fold_in(own, 4), (number_of // 2,), 0, 1 << 20) % (slack + 1)
    lengths = lengths.at[source_of].add(-shifted).at[sink].add(shifted)
    labels = jnp.searchsorted(jnp.cumsum(lengths), jnp.arange(rows * top), side="right").astype(jnp.int32)
    table = labels.reshape(top, rows).T
    table = table[jax.random.permutation(jax.random.fold_in(own, 1), rows)]
    turn = jax.random.randint(jax.random.fold_in(own, 2), (rows, 1), 0, top)
    return jnp.take_along_axis(table, (jnp.arange(top)[None, :] + turn) % top, axis=1)


def portions_of(amount, total, reach, skew, full):
    loads = [(1 << 20) // math.isqrt(standing ** skew) + 1 for standing in range(1, amount + 1)]
    largest = reach if full else min(reach, max(-(-total // amount), total * loads[0] // sum(loads)))
    least = 1 if total - largest >= amount - 1 else 0
    given, surplus = [largest] + [least] * (amount - 1), total - largest - least * (amount - 1)
    while surplus > 0:
        movable = [i for i in range(1, amount) if given[i] < largest] or [i for i in range(1, amount) if given[i] < reach]
        pool, budget = sum([loads[i] for i in movable]), surplus
        for i in movable:
            extra = min(reach - given[i], max(1, budget * loads[i] // pool), surplus)
            given[i] = given[i] + extra
            surplus = surplus - extra
    return np.array(given)


def bell_draw(key, extent, spread, bound, split=(), kind=jnp.bfloat16):
    result = jax.random.normal(key, extent, jnp.float32) * spread
    if len(split) > 0:
        result = shard_levels(key, extent, split, -0.22, 0.18) * result
    return jnp.clip(result, min=-bound, max=bound).astype(kind)


def setup_inputs(seed: int = 0) -> dict:
    seeds = jax.random.split(jax.random.key(seed), 4)
    spectra = bell_draw(seeds[0], (SPECTRA, BINS), 1.0, 6.0, ((0, 128),))
    window_keys = jax.random.split(jax.random.fold_in(seeds[1], 1), SPECTRA // S_DEV)
    window_turns = jax.random.permutation(jax.random.fold_in(seeds[1], 3), SPECTRA // S_DEV)
    window = jax.vmap(lambda own, number: assign_block(jax.random.fold_in(seeds[1], 2), own, number, S_DEV, N_MASS, 1, CAP, 2))(window_keys, window_turns).reshape((SPECTRA, 1))
    cluster = place_ends(jax.random.randint(seeds[2], (SPECTRA,), 0, CL_WIN), jax.random.fold_in(seeds[2], 1), 0, CL_WIN - 1).astype(jnp.int32)
    return dict(spectra=spectra, window=window, cluster=cluster)


def reference(spectra, window, cluster):
    values = spectra.astype(jnp.float32)
    scaled = (values * lax.rsqrt(lax.optimization_barrier(jnp.mean(values * values, axis=1, keepdims=True)) + 1e-06)).astype(jnp.bfloat16)
    target = window[:, 0].astype(jnp.int32)
    per_device = target.reshape(N_MASS * N_TILE, S_DEV)
    member = (per_device[:, :, None] == jnp.arange(N_MASS, dtype=jnp.int32)[None, None, :]).astype(jnp.int32)
    before = jnp.cumsum(member, axis=1) - member
    slot_rank = lax.optimization_barrier(jnp.sum(before * member, axis=2)).reshape(-1).astype(jnp.int32)
    source = jnp.arange(SPECTRA, dtype=jnp.int32) // S_DEV
    column = source % N_TILE * SLOTS + source // N_TILE * CAP + slot_rank
    placed = jnp.zeros((N_MASS, GROUP, BINS), jnp.bfloat16).at[target, column].set(scaled)

    def group_gram(block_rows):
        return jnp.dot(block_rows, block_rows.T, preferred_element_type=jnp.float32) * (1.0 / BINS)
    gram_tiles = lax.map(group_gram, placed).reshape(N_MASS * GROUP, GROUP)
    global_cluster = (target * CL_WIN + cluster.astype(jnp.int32)).astype(jnp.int32)
    consensus = jax.ops.segment_sum(scaled.astype(jnp.float32), global_cluster, num_segments=CLUSTERS)
    return (gram_tiles, consensus)
```

```python
import jax
import jax.numpy as jnp
from jax import lax
from jax.sharding import PartitionSpec as P

CL_DEV = 4


def shards(spectra, window, cluster):
    s_dev, num_bins = spectra.shape
    mass_count = lax.axis_size("mass")
    tile_count = lax.axis_size("tile")
    per_window = CL_DEV * tile_count
    capacity = 2 * s_dev // mass_count
    slot_count = mass_count * capacity
    values = spectra.astype(jnp.float32)
    scaled = (values * lax.rsqrt(jnp.mean(values * values, axis=1, keepdims=True) + 1e-06)).astype(
        jnp.bfloat16
    )
    target = window[:, 0]
    global_ids = target * per_window + cluster
    member = (target[:, None] == jnp.arange(mass_count, dtype=jnp.int32)[None, :]).astype(jnp.int32)
    before = jnp.cumsum(member, axis=0) - member
    slot_rank = jnp.sum(before * member, axis=1)
    position = target * capacity + slot_rank
    chosen = jnp.arange(slot_count, dtype=jnp.int32)[:, None] == position[None, :]
    outgoing = jnp.dot(
        chosen.astype(jnp.bfloat16), scaled, preferred_element_type=jnp.float32
    ).astype(jnp.bfloat16)
    outgoing = outgoing.reshape(mass_count, capacity, num_bins)
    labels = jnp.max(jnp.where(chosen, global_ids[None, :], -1), axis=1).reshape(
        mass_count, capacity
    )
    arrived, arrived_labels = (
        lax.all_to_all(outgoing, "mass", split_axis=0, concat_axis=0, tiled=True),
        lax.all_to_all(labels, "mass", split_axis=0, concat_axis=0, tiled=True),
    )
    arrived = arrived.reshape(slot_count, num_bins)
    arrived_labels = arrived_labels.reshape(slot_count)
    gathered = lax.all_gather(arrived, "tile", axis=0, tiled=True)
    gathered_labels = lax.all_gather(arrived_labels, "tile", axis=0, tiled=True)
    product = lax.dot_general(
        arrived,
        gathered,
        (((1,), (1,)), ((), ())),
        preferred_element_type=jnp.float32,
    )
    gram_tiles = product * (1.0 / num_bins)
    own_ids = (
        lax.axis_index("mass") * per_window
        + lax.axis_index("tile") * CL_DEV
        + jnp.arange(CL_DEV, dtype=jnp.int32)
    )
    one_hot = (own_ids[:, None] == gathered_labels[None, :]).astype(jnp.bfloat16)
    consensus = jnp.dot(one_hot, gathered, preferred_element_type=jnp.float32)
    return (gram_tiles, consensus)


def solution(mesh):
    in_specs = (P(("mass", "tile"), None), P(("mass", "tile"), None), P(("mass", "tile")))
    out_specs = (P(("mass", "tile"), None), P(("mass", "tile"), None))
    return jax.shard_map(shards, mesh=mesh, in_specs=in_specs, out_specs=out_specs, check_vma=False)
```

```python
import jax
import jax.numpy as jnp
from jax import lax
from jax.sharding import PartitionSpec as P


CL_DEV = 4
CHUNKS = 4
LABEL_COLS = 128


def shards(spectra, window, cluster):
    s_dev, num_bins = spectra.shape
    mass_count = lax.axis_size("mass")
    capacity = 2 * s_dev // mass_count
    slot_count = mass_count * capacity
    values = spectra.astype(jnp.float32)
    scaled = (values * lax.rsqrt(jnp.mean(values * values, axis=1, keepdims=True) + 1e-06)).astype(
        jnp.bfloat16
    )
    target = window[:, 0]
    member = (target[:, None] == jnp.arange(mass_count, dtype=jnp.int32)[None, :]).astype(jnp.int32)
    before = jnp.cumsum(member, axis=0) - member
    slot_rank = jnp.sum(before * member, axis=1)
    position = target * capacity + slot_rank
    chosen = jnp.arange(slot_count, dtype=jnp.int32)[:, None] == position[None, :]
    tagged = jnp.concatenate(
        [
            jnp.broadcast_to(cluster[:, None].astype(jnp.bfloat16), (s_dev, LABEL_COLS)),
            scaled,
        ],
        axis=1,
    )
    outgoing = jnp.dot(
        chosen.astype(jnp.bfloat16), tagged, preferred_element_type=jnp.float32
    ).astype(jnp.bfloat16)
    empty = jnp.logical_not(jnp.any(chosen, axis=1))
    outgoing = outgoing.at[:, :LABEL_COLS].set(
        jnp.where(empty[:, None], jnp.bfloat16(-1), outgoing[:, :LABEL_COLS])
    )
    outgoing = outgoing.reshape(mass_count, capacity, LABEL_COLS + num_bins)
    own_ids = lax.axis_index("tile") * CL_DEV + jnp.arange(CL_DEV, dtype=jnp.int32)

    chunk = num_bins // CHUNKS
    gram = None
    one_hot = None
    consensus_parts = []
    for j in range(CHUNKS):
        lo = 0 if j == 0 else LABEL_COLS + j * chunk
        hi = LABEL_COLS + (j + 1) * chunk
        piece = outgoing[:, :, lo:hi]
        arrived = lax.all_to_all(piece, "mass", split_axis=0, concat_axis=0, tiled=True)
        arrived = arrived.reshape(slot_count, hi - lo)
        gathered = lax.all_gather(arrived, "tile", axis=0, tiled=True)
        if j == 0:
            labels = gathered[:, 0].astype(jnp.int32)
            one_hot = (own_ids[:, None] == labels[None, :]).astype(jnp.bfloat16)
            arrived = arrived[:, LABEL_COLS:]
            gathered = gathered[:, LABEL_COLS:]
        part = lax.dot_general(
            arrived, gathered, (((1,), (1,)), ((), ())), preferred_element_type=jnp.float32
        ) * (1.0 / num_bins)
        gram = lax.optimization_barrier(part if gram is None else gram + part)
        consensus_parts.append(jnp.dot(one_hot, gathered, preferred_element_type=jnp.float32))
    gram_tiles = gram
    consensus = jnp.concatenate(consensus_parts, axis=1)
    return (gram_tiles, consensus)


def solution(mesh):
    in_specs = (P(("mass", "tile"), None), P(("mass", "tile"), None), P(("mass", "tile")))
    out_specs = (P(("mass", "tile"), None), P(("mass", "tile"), None))
    return jax.shard_map(shards, mesh=mesh, in_specs=in_specs, out_specs=out_specs, check_vma=False)
```

```python
import jax
import jax.numpy as jnp
from jax import lax
from jax.sharding import PartitionSpec as P


CL_DEV = 4


def shards(spectra, window, cluster):
    s_dev, num_bins = spectra.shape
    mass_count = lax.axis_size("mass")
    tile_count = lax.axis_size("tile")
    per_window = CL_DEV * tile_count
    capacity = 2 * s_dev // mass_count
    slot_count = mass_count * capacity
    values = spectra.astype(jnp.float32)
    scaled = (values * lax.rsqrt(jnp.mean(values * values, axis=1, keepdims=True) + 1e-06)).astype(
        jnp.bfloat16
    )
    target = window[:, 0]
    global_ids = target * per_window + cluster
    member = (target[:, None] == jnp.arange(mass_count, dtype=jnp.int32)[None, :]).astype(jnp.int32)
    before = jnp.cumsum(member, axis=0) - member
    slot_rank = jnp.sum(before * member, axis=1)
    position = target * capacity + slot_rank
    chosen = jnp.arange(slot_count, dtype=jnp.int32)[:, None] == position[None, :]
    outgoing = jnp.dot(
        chosen.astype(jnp.bfloat16), scaled, preferred_element_type=jnp.float32
    ).astype(jnp.bfloat16)
    outgoing = outgoing.reshape(mass_count, capacity, num_bins)
    labels = jnp.max(jnp.where(chosen, global_ids[None, :], -1), axis=1).reshape(
        mass_count, capacity
    )
    arrived, arrived_labels = (
        lax.all_to_all(outgoing, "mass", split_axis=0, concat_axis=0, tiled=True),
        lax.all_to_all(labels, "mass", split_axis=0, concat_axis=0, tiled=True),
    )
    arrived = arrived.reshape(slot_count, num_bins)
    arrived_labels = arrived_labels.reshape(slot_count)
    tile_count = lax.axis_size("tile")
    local_labels = arrived_labels - lax.axis_index("mass") * per_window
    cluster_ids = jnp.arange(per_window, dtype=jnp.int32)
    one_hot = (cluster_ids[:, None] == local_labels[None, :]).astype(jnp.bfloat16)
    gathered = lax.all_gather(arrived, "tile", axis=0, tiled=True)
    partial = jnp.dot(one_hot, arrived, preferred_element_type=jnp.float32)
    pieces = lax.all_to_all(
        partial.reshape(tile_count, CL_DEV, num_bins), "tile", split_axis=0, concat_axis=0, tiled=True
    )
    consensus = jnp.sum(pieces, axis=0)
    product = lax.dot_general(
        arrived,
        gathered,
        (((1,), (1,)), ((), ())),
        preferred_element_type=jnp.float32,
    )
    gram_tiles = product * (1.0 / num_bins)
    return (gram_tiles, consensus)


def solution(mesh):
    in_specs = (P(("mass", "tile"), None), P(("mass", "tile"), None), P(("mass", "tile")))
    out_specs = (P(("mass", "tile"), None), P(("mass", "tile"), None))
    return jax.shard_map(shards, mesh=mesh, in_specs=in_specs, out_specs=out_specs, check_vma=False)
```

```python
import functools

import jax
import jax.numpy as jnp
from jax import lax
from jax.experimental import pallas as pl
from jax.experimental.pallas import tpu as pltpu
from jax.sharding import PartitionSpec as P

CL_DEV = 4
ONE_HOT_ROWS = 8

def _gram_consensus_kernel(scale, a_ref, oh_ref, p_ref, g_ref, c_ref):
    j = pl.program_id(0)
    blk = p_ref[...]
    g_ref[...] = lax.dot_general(
        a_ref[...], blk, (((1,), (1,)), ((), ())), preferred_element_type=jnp.float32
    ) * scale

    @pl.when(j == 0)
    def _():
        c_ref[...] = jnp.zeros_like(c_ref)

    c_ref[...] += jnp.dot(oh_ref[...], blk, preferred_element_type=jnp.float32)


def gram_consensus(arrived, one_hot, gathered, block_rows=1024):
    rows, bins = arrived.shape
    total = gathered.shape[0]
    heads = one_hot.shape[0]
    steps = total // block_rows
    flops = 2 * rows * total * bins + 2 * heads * total * bins
    bytes_accessed = 2 * (rows * bins + heads * total + total * bins) + 4 * (rows * total + heads * bins)
    return pl.pallas_call(
        functools.partial(_gram_consensus_kernel, 1.0 / bins),
        grid=(steps,),
        in_specs=[
            pl.BlockSpec((rows, bins), lambda j: (0, 0)),
            pl.BlockSpec((heads, block_rows), lambda j: (0, j)),
            pl.BlockSpec((block_rows, bins), lambda j: (j, 0)),
        ],
        out_specs=[
            pl.BlockSpec((rows, block_rows), lambda j: (0, j)),
            pl.BlockSpec((heads, bins), lambda j: (0, 0)),
        ],
        out_shape=[
            jax.ShapeDtypeStruct((rows, total), jnp.float32),
            jax.ShapeDtypeStruct((heads, bins), jnp.float32),
        ],
        compiler_params=pltpu.CompilerParams(dimension_semantics=("arbitrary",)),
        cost_estimate=pl.CostEstimate(flops=flops, bytes_accessed=bytes_accessed, transcendentals=0),
    )(arrived, one_hot, gathered)


def shards(spectra, window, cluster):
    s_dev, num_bins = spectra.shape
    mass_count = lax.axis_size("mass")
    tile_count = lax.axis_size("tile")
    per_window = CL_DEV * tile_count
    capacity = 2 * s_dev // mass_count
    slot_count = mass_count * capacity
    values = spectra.astype(jnp.float32)
    scaled = (values * lax.rsqrt(jnp.mean(values * values, axis=1, keepdims=True) + 1e-06)).astype(
        jnp.bfloat16
    )
    target = window[:, 0]
    global_ids = target * per_window + cluster
    member = (target[:, None] == jnp.arange(mass_count, dtype=jnp.int32)[None, :]).astype(jnp.int32)
    before = jnp.cumsum(member, axis=0) - member
    slot_rank = jnp.sum(before * member, axis=1)
    position = target * capacity + slot_rank
    chosen = jnp.arange(slot_count, dtype=jnp.int32)[:, None] == position[None, :]
    outgoing = jnp.dot(
        chosen.astype(jnp.bfloat16), scaled, preferred_element_type=jnp.float32
    ).astype(jnp.bfloat16)
    outgoing = outgoing.reshape(mass_count, capacity, num_bins)
    labels = jnp.max(jnp.where(chosen, global_ids[None, :], -1), axis=1).reshape(
        mass_count, capacity
    )
    arrived, arrived_labels = (
        lax.all_to_all(outgoing, "mass", split_axis=0, concat_axis=0, tiled=True),
        lax.all_to_all(labels, "mass", split_axis=0, concat_axis=0, tiled=True),
    )
    arrived = arrived.reshape(slot_count, num_bins)
    arrived_labels = arrived_labels.reshape(slot_count)
    gathered = lax.all_gather(arrived, "tile", axis=0, tiled=True)
    gathered_labels = lax.all_gather(arrived_labels, "tile", axis=0, tiled=True)
    own_ids = (
        lax.axis_index("mass") * per_window
        + lax.axis_index("tile") * CL_DEV
        + jnp.arange(ONE_HOT_ROWS, dtype=jnp.int32)
    )
    own_ids = jnp.where(jnp.arange(ONE_HOT_ROWS) < CL_DEV, own_ids, -2)
    one_hot = (own_ids[:, None] == gathered_labels[None, :]).astype(jnp.bfloat16)
    gram_tiles, consensus = gram_consensus(arrived, one_hot, gathered)
    consensus = consensus[:CL_DEV]
    return (gram_tiles, consensus)


def solution(mesh):
    in_specs = (P(("mass", "tile"), None), P(("mass", "tile"), None), P(("mass", "tile")))
    out_specs = (P(("mass", "tile"), None), P(("mass", "tile"), None))
    return jax.shard_map(shards, mesh=mesh, in_specs=in_specs, out_specs=out_specs, check_vma=False)
```

```python
import functools

import jax
import jax.numpy as jnp
from jax import lax
from jax.experimental import pallas as pl
from jax.experimental.pallas import tpu as pltpu
from jax.sharding import PartitionSpec as P

CL_DEV = 4
ONE_HOT_ROWS = 4

def _gram_consensus_kernel(scale, a_ref, oh_ref, p_ref, g_ref, c_ref):
    j = pl.program_id(0)
    blk = p_ref[...]
    g_ref[...] = lax.dot_general(
        a_ref[...], blk, (((1,), (1,)), ((), ())), preferred_element_type=jnp.float32
    ) * scale

    @pl.when(j == 0)
    def _():
        c_ref[...] = jnp.zeros_like(c_ref)

    c_ref[...] += jnp.dot(oh_ref[...], blk, preferred_element_type=jnp.float32)


def gram_consensus(arrived, one_hot, gathered, block_rows=1024):
    rows, bins = arrived.shape
    total = gathered.shape[0]
    heads = one_hot.shape[0]
    steps = total // block_rows
    flops = 2 * rows * total * bins + 2 * heads * total * bins
    bytes_accessed = 2 * (rows * bins + heads * total + total * bins) + 4 * (rows * total + heads * bins)
    return pl.pallas_call(
        functools.partial(_gram_consensus_kernel, 1.0 / bins),
        grid=(steps,),
        in_specs=[
            pl.BlockSpec((rows, bins), lambda j: (0, 0)),
            pl.BlockSpec((heads, block_rows), lambda j: (0, j)),
            pl.BlockSpec((block_rows, bins), lambda j: (j, 0)),
        ],
        out_specs=[
            pl.BlockSpec((rows, block_rows), lambda j: (0, j)),
            pl.BlockSpec((heads, bins), lambda j: (0, 0)),
        ],
        out_shape=[
            jax.ShapeDtypeStruct((rows, total), jnp.float32),
            jax.ShapeDtypeStruct((heads, bins), jnp.float32),
        ],
        compiler_params=pltpu.CompilerParams(dimension_semantics=("arbitrary",)),
        cost_estimate=pl.CostEstimate(flops=flops, bytes_accessed=bytes_accessed, transcendentals=0),
    )(arrived, one_hot, gathered)


def exchange_over_mass(pieces, mass_count):
    me = lax.axis_index("mass")
    held = [pieces[me]]
    for shift in range(1, mass_count):
        perm = [(i, (i + shift) % mass_count) for i in range(mass_count)]
        held.append(lax.ppermute(pieces[(me + shift) % mass_count], "mass", perm))
    stacked = jnp.stack(held)
    return stacked[(me - jnp.arange(mass_count)) % mass_count]


def shards(spectra, window, cluster):
    s_dev, num_bins = spectra.shape
    mass_count = lax.axis_size("mass")
    tile_count = lax.axis_size("tile")
    per_window = CL_DEV * tile_count
    capacity = 2 * s_dev // mass_count
    slot_count = mass_count * capacity
    values = spectra.astype(jnp.float32)
    scaled = (values * lax.rsqrt(jnp.mean(values * values, axis=1, keepdims=True) + 1e-06)).astype(
        jnp.bfloat16
    )
    target = window[:, 0]
    global_ids = target * per_window + cluster
    member = (target[:, None] == jnp.arange(mass_count, dtype=jnp.int32)[None, :]).astype(jnp.int32)
    before = jnp.cumsum(member, axis=0) - member
    slot_rank = jnp.sum(before * member, axis=1)
    position = target * capacity + slot_rank
    chosen = jnp.arange(slot_count, dtype=jnp.int32)[:, None] == position[None, :]
    outgoing = jnp.dot(
        chosen.astype(jnp.bfloat16), scaled, preferred_element_type=jnp.float32
    ).astype(jnp.bfloat16)
    outgoing = outgoing.reshape(mass_count, capacity, num_bins)
    labels = jnp.max(jnp.where(chosen, global_ids[None, :], -1), axis=1).reshape(
        mass_count, capacity
    )
    arrived = exchange_over_mass(outgoing, mass_count)
    arrived_labels = exchange_over_mass(labels, mass_count)
    arrived = arrived.reshape(slot_count, num_bins)
    arrived_labels = arrived_labels.reshape(slot_count)
    gathered = lax.all_gather(arrived, "tile", axis=0, tiled=True)
    gathered_labels = lax.all_gather(arrived_labels, "tile", axis=0, tiled=True)
    own_ids = (
        lax.axis_index("mass") * per_window
        + lax.axis_index("tile") * CL_DEV
        + jnp.arange(ONE_HOT_ROWS, dtype=jnp.int32)
    )
    one_hot = (own_ids[:, None] == gathered_labels[None, :]).astype(jnp.bfloat16)
    gram_tiles, consensus = gram_consensus(arrived, one_hot, gathered)
    return (gram_tiles, consensus)


def solution(mesh):
    in_specs = (P(("mass", "tile"), None), P(("mass", "tile"), None), P(("mass", "tile")))
    out_specs = (P(("mass", "tile"), None), P(("mass", "tile"), None))
    return jax.shard_map(shards, mesh=mesh, in_specs=in_specs, out_specs=out_specs, check_vma=False)
```

```python
import functools

import jax
import jax.numpy as jnp
from jax import lax
from jax.experimental import pallas as pl
from jax.experimental.pallas import tpu as pltpu
from jax.sharding import PartitionSpec as P

CL_DEV = 4
ONE_HOT_ROWS = 4

def _gram_consensus_kernel(scale, a_ref, oh_ref, p_ref, g_ref, c_ref):
    j = pl.program_id(0)
    blk = p_ref[...]
    g_ref[...] = lax.dot_general(
        a_ref[...], blk, (((1,), (1,)), ((), ())), preferred_element_type=jnp.float32
    ) * scale

    @pl.when(j == 0)
    def _():
        c_ref[...] = jnp.zeros_like(c_ref)

    c_ref[...] += jnp.dot(oh_ref[...], blk, preferred_element_type=jnp.float32)


def gram_consensus(arrived, one_hot, gathered, block_rows=1024):
    rows, bins = arrived.shape
    total = gathered.shape[0]
    heads = one_hot.shape[0]
    steps = total // block_rows
    flops = 2 * rows * total * bins + 2 * heads * total * bins
    bytes_accessed = 2 * (rows * bins + heads * total + total * bins) + 4 * (rows * total + heads * bins)
    return pl.pallas_call(
        functools.partial(_gram_consensus_kernel, 1.0 / bins),
        grid=(steps,),
        in_specs=[
            pl.BlockSpec((rows, bins), lambda j: (0, 0)),
            pl.BlockSpec((heads, block_rows), lambda j: (0, j)),
            pl.BlockSpec((block_rows, bins), lambda j: (j, 0)),
        ],
        out_specs=[
            pl.BlockSpec((rows, block_rows), lambda j: (0, j)),
            pl.BlockSpec((heads, bins), lambda j: (0, 0)),
        ],
        out_shape=[
            jax.ShapeDtypeStruct((rows, total), jnp.float32),
            jax.ShapeDtypeStruct((heads, bins), jnp.float32),
        ],
        compiler_params=pltpu.CompilerParams(dimension_semantics=("arbitrary",)),
        cost_estimate=pl.CostEstimate(flops=flops, bytes_accessed=bytes_accessed, transcendentals=0),
    )(arrived, one_hot, gathered)


def exchange_over_mass(pieces, mass_count):
    me = lax.axis_index("mass")
    ahead = [(i, (i + 1) % mass_count) for i in range(mass_count)]
    behind = [(i, (i - 1) % mass_count) for i in range(mass_count)]
    from_behind = lax.ppermute(pieces[(me + 1) % mass_count], "mass", ahead)
    from_ahead = lax.ppermute(pieces[(me - 1) % mass_count], "mass", behind)
    far = pieces[(me + 2) % mass_count]
    half = far.shape[0] // 2
    first = lax.ppermute(lax.ppermute(far[:half], "mass", ahead), "mass", ahead)
    second = lax.ppermute(lax.ppermute(far[half:], "mass", behind), "mass", behind)
    opposite = jnp.concatenate([first, second], axis=0)
    stacked = jnp.stack([pieces[me], from_behind, opposite, from_ahead])
    return stacked[(me - jnp.arange(mass_count)) % mass_count]


def shards(spectra, window, cluster):
    s_dev, num_bins = spectra.shape
    mass_count = lax.axis_size("mass")
    tile_count = lax.axis_size("tile")
    per_window = CL_DEV * tile_count
    capacity = 2 * s_dev // mass_count
    slot_count = mass_count * capacity
    values = spectra.astype(jnp.float32)
    scaled = (values * lax.rsqrt(jnp.mean(values * values, axis=1, keepdims=True) + 1e-06)).astype(
        jnp.bfloat16
    )
    target = window[:, 0]
    global_ids = target * per_window + cluster
    member = (target[:, None] == jnp.arange(mass_count, dtype=jnp.int32)[None, :]).astype(jnp.int32)
    before = jnp.cumsum(member, axis=0) - member
    slot_rank = jnp.sum(before * member, axis=1)
    position = target * capacity + slot_rank
    chosen = jnp.arange(slot_count, dtype=jnp.int32)[:, None] == position[None, :]
    outgoing = jnp.dot(
        chosen.astype(jnp.bfloat16), scaled, preferred_element_type=jnp.float32
    ).astype(jnp.bfloat16)
    outgoing = outgoing.reshape(mass_count, capacity, num_bins)
    labels = jnp.max(jnp.where(chosen, global_ids[None, :], -1), axis=1).reshape(
        mass_count, capacity
    )
    arrived = exchange_over_mass(outgoing, mass_count)
    arrived_labels = exchange_over_mass(labels, mass_count)
    arrived = arrived.reshape(slot_count, num_bins)
    arrived_labels = arrived_labels.reshape(slot_count)
    gathered = lax.all_gather(arrived, "tile", axis=0, tiled=True)
    gathered_labels = lax.all_gather(arrived_labels, "tile", axis=0, tiled=True)
    own_ids = (
        lax.axis_index("mass") * per_window
        + lax.axis_index("tile") * CL_DEV
        + jnp.arange(ONE_HOT_ROWS, dtype=jnp.int32)
    )
    one_hot = (own_ids[:, None] == gathered_labels[None, :]).astype(jnp.bfloat16)
    gram_tiles, consensus = gram_consensus(arrived, one_hot, gathered)
    return (gram_tiles, consensus)


def solution(mesh):
    in_specs = (P(("mass", "tile"), None), P(("mass", "tile"), None), P(("mass", "tile")))
    out_specs = (P(("mass", "tile"), None), P(("mass", "tile"), None))
    return jax.shard_map(shards, mesh=mesh, in_specs=in_specs, out_specs=out_specs, check_vma=False)
```

```python
import functools

import jax
import jax.numpy as jnp
from jax import lax
from jax.experimental import pallas as pl
from jax.experimental.pallas import tpu as pltpu
from jax.sharding import PartitionSpec as P

CL_DEV = 4

def _gram_consensus_kernel(scale, rows, half_ref, a_ref, oh_ref, p_ref, mine_ref, theirs_ref, c_ref):
    j = pl.program_id(0)
    blk = p_ref[...]
    res = lax.dot_general(
        a_ref[...], blk, (((1,), (1,)), ((), ())), preferred_element_type=jnp.float32
    ) * scale
    mine_ref[...] = res[:rows]
    theirs_ref[...] = res[rows:]

    @pl.when(j == 0)
    def _():
        c_ref[...] = jnp.zeros_like(c_ref)

    c_ref[...] += jnp.dot(oh_ref[...], blk, preferred_element_type=jnp.float32)


def gram_consensus(half, pair_rows, one_hot, gathered, block_rows=1024):
    rows = pair_rows.shape[0] // 2
    bins = pair_rows.shape[1]
    total = gathered.shape[0]
    heads = one_hot.shape[0]
    steps = total // 2 // block_rows
    flops = 2 * 2 * rows * (total // 2) * bins + 2 * heads * (total // 2) * bins
    bytes_accessed = 2 * (2 * rows * bins + heads * total // 2 + total // 2 * bins) + 4 * (
        2 * rows * total // 2 + heads * bins
    )
    grid_spec = pltpu.PrefetchScalarGridSpec(
        num_scalar_prefetch=1,
        grid=(steps,),
        in_specs=[
            pl.BlockSpec((2 * rows, bins), lambda j, h: (0, 0)),
            pl.BlockSpec((heads, block_rows), lambda j, h: (0, h[0] * steps + j)),
            pl.BlockSpec((block_rows, bins), lambda j, h: (h[0] * steps + j, 0)),
        ],
        out_specs=[
            pl.BlockSpec((rows, block_rows), lambda j, h: (0, h[0] * steps + j)),
            pl.BlockSpec((rows, block_rows), lambda j, h: (0, j)),
            pl.BlockSpec((heads, bins), lambda j, h: (0, 0)),
        ],
    )
    return pl.pallas_call(
        functools.partial(_gram_consensus_kernel, 1.0 / bins, rows),
        grid_spec=grid_spec,
        out_shape=[
            jax.ShapeDtypeStruct((rows, total), jnp.float32),
            jax.ShapeDtypeStruct((rows, total // 2), jnp.float32),
            jax.ShapeDtypeStruct((heads, bins), jnp.float32),
        ],
        compiler_params=pltpu.CompilerParams(dimension_semantics=("arbitrary",)),
        cost_estimate=pl.CostEstimate(flops=flops, bytes_accessed=bytes_accessed, transcendentals=0),
    )(half, pair_rows, one_hot, gathered)


def exchange_over_mass(pieces, mass_count):
    me = lax.axis_index("mass")
    ahead = [(i, (i + 1) % mass_count) for i in range(mass_count)]
    behind = [(i, (i - 1) % mass_count) for i in range(mass_count)]
    from_behind = lax.ppermute(pieces[(me + 1) % mass_count], "mass", ahead)
    from_ahead = lax.ppermute(pieces[(me - 1) % mass_count], "mass", behind)
    far = pieces[(me + 2) % mass_count]
    half = far.shape[0] // 2
    first = lax.ppermute(lax.ppermute(far[:half], "mass", ahead), "mass", ahead)
    second = lax.ppermute(lax.ppermute(far[half:], "mass", behind), "mass", behind)
    opposite = jnp.concatenate([first, second], axis=0)
    stacked = jnp.stack([pieces[me], from_behind, opposite, from_ahead])
    return stacked[(me - jnp.arange(mass_count)) % mass_count]


def shards(spectra, window, cluster):
    s_dev, num_bins = spectra.shape
    mass_count = lax.axis_size("mass")
    tile_count = lax.axis_size("tile")
    per_window = CL_DEV * tile_count
    capacity = 2 * s_dev // mass_count
    slot_count = mass_count * capacity
    values = spectra.astype(jnp.float32)
    scaled = (values * lax.rsqrt(jnp.mean(values * values, axis=1, keepdims=True) + 1e-06)).astype(
        jnp.bfloat16
    )
    target = window[:, 0]
    global_ids = target * per_window + cluster
    member = (target[:, None] == jnp.arange(mass_count, dtype=jnp.int32)[None, :]).astype(jnp.int32)
    before = jnp.cumsum(member, axis=0) - member
    slot_rank = jnp.sum(before * member, axis=1)
    position = target * capacity + slot_rank
    chosen = jnp.arange(slot_count, dtype=jnp.int32)[:, None] == position[None, :]
    outgoing = jnp.dot(
        chosen.astype(jnp.bfloat16), scaled, preferred_element_type=jnp.float32
    ).astype(jnp.bfloat16)
    outgoing = outgoing.reshape(mass_count, capacity, num_bins)
    labels = jnp.max(jnp.where(chosen, global_ids[None, :], -1), axis=1).reshape(
        mass_count, capacity
    )
    arrived = exchange_over_mass(outgoing, mass_count)
    arrived_labels = exchange_over_mass(labels, mass_count)
    arrived = arrived.reshape(slot_count, num_bins)
    arrived_labels = arrived_labels.reshape(slot_count)
    gathered = lax.all_gather(arrived, "tile", axis=0, tiled=True)
    gathered_labels = lax.all_gather(arrived_labels, "tile", axis=0, tiled=True)
    tile = lax.axis_index("tile")
    swap = [(i, i ^ 1) for i in range(tile_count)]
    half = tile % 2
    partner_rows = lax.ppermute(arrived, "tile", swap)
    pair_rows = jnp.concatenate([arrived, partner_rows], axis=0)
    owners = jnp.where(jnp.arange(2 * CL_DEV) < CL_DEV, tile, tile ^ 1)
    own_ids = (
        lax.axis_index("mass") * per_window
        + owners * CL_DEV
        + jnp.arange(2 * CL_DEV, dtype=jnp.int32) % CL_DEV
    )
    one_hot = (own_ids[:, None] == gathered_labels[None, :]).astype(jnp.bfloat16)
    mine, theirs, sums = gram_consensus(half.reshape(1), pair_rows, one_hot, gathered)
    returned = lax.ppermute(theirs, "tile", swap)
    gram_tiles = lax.dynamic_update_slice(mine, returned, (0, (1 - half) * theirs.shape[1]))
    consensus = sums[:CL_DEV] + lax.ppermute(sums[CL_DEV:], "tile", swap)
    return (gram_tiles, consensus)


def solution(mesh):
    in_specs = (P(("mass", "tile"), None), P(("mass", "tile"), None), P(("mass", "tile")))
    out_specs = (P(("mass", "tile"), None), P(("mass", "tile"), None))
    return jax.shard_map(shards, mesh=mesh, in_specs=in_specs, out_specs=out_specs, check_vma=False)
```

```python
import functools

import jax
import jax.numpy as jnp
from jax import lax
from jax.experimental import pallas as pl
from jax.experimental.pallas import tpu as pltpu
from jax.sharding import PartitionSpec as P

CL_DEV = 4

def _gram_consensus_kernel(scale, rows, half_ref, a_ref, oh_ref, p_ref, prior_ref, mine_ref, theirs_ref, c_ref):
    del prior_ref
    j = pl.program_id(0)
    blk = p_ref[...]
    res = lax.dot_general(
        a_ref[...], blk, (((1,), (1,)), ((), ())), preferred_element_type=jnp.float32
    ) * scale
    mine_ref[...] = res[:rows]
    theirs_ref[...] = res[rows:]

    @pl.when(j == 0)
    def _():
        c_ref[...] = jnp.zeros_like(c_ref)

    c_ref[...] += jnp.dot(oh_ref[...], blk, preferred_element_type=jnp.float32)


def gram_consensus(half, part, parts, pair_rows, one_hot, gathered, prior, block_rows=512):
    rows = pair_rows.shape[0] // 2
    bins = pair_rows.shape[1]
    total = gathered.shape[0]
    heads = one_hot.shape[0]
    width = total // 2 // parts
    steps = width // block_rows
    per_half = total // 2 // block_rows
    first = part * steps
    flops = 2 * 2 * rows * width * bins + 2 * heads * width * bins
    bytes_accessed = 2 * (2 * rows * bins + heads * width + width * bins) + 4 * (2 * rows * width + heads * bins)
    grid_spec = pltpu.PrefetchScalarGridSpec(
        num_scalar_prefetch=1,
        grid=(steps,),
        in_specs=[
            pl.BlockSpec((2 * rows, bins), lambda j, h: (0, 0)),
            pl.BlockSpec((heads, block_rows), lambda j, h: (0, h[0] * per_half + first + j)),
            pl.BlockSpec((block_rows, bins), lambda j, h: (h[0] * per_half + first + j, 0)),
            pl.BlockSpec(memory_space=pl.ANY),
        ],
        out_specs=[
            pl.BlockSpec((rows, block_rows), lambda j, h: (0, h[0] * per_half + first + j)),
            pl.BlockSpec((rows, block_rows), lambda j, h: (0, j)),
            pl.BlockSpec((heads, bins), lambda j, h: (0, 0)),
        ],
    )
    return pl.pallas_call(
        functools.partial(_gram_consensus_kernel, 1.0 / bins, rows),
        grid_spec=grid_spec,
        out_shape=[
            jax.ShapeDtypeStruct((rows, total), jnp.float32),
            jax.ShapeDtypeStruct((rows, width), jnp.float32),
            jax.ShapeDtypeStruct((heads, bins), jnp.float32),
        ],
        input_output_aliases={4: 0},
        compiler_params=pltpu.CompilerParams(dimension_semantics=("arbitrary",)),
        cost_estimate=pl.CostEstimate(flops=flops, bytes_accessed=bytes_accessed, transcendentals=0),
    )(half, pair_rows, one_hot, gathered, prior)


def exchange_over_mass(pieces, mass_count):
    me = lax.axis_index("mass")
    ahead = [(i, (i + 1) % mass_count) for i in range(mass_count)]
    behind = [(i, (i - 1) % mass_count) for i in range(mass_count)]
    from_behind = lax.ppermute(pieces[(me + 1) % mass_count], "mass", ahead)
    from_ahead = lax.ppermute(pieces[(me - 1) % mass_count], "mass", behind)
    far = pieces[(me + 2) % mass_count]
    half = far.shape[0] // 2
    first = lax.ppermute(lax.ppermute(far[:half], "mass", ahead), "mass", ahead)
    second = lax.ppermute(lax.ppermute(far[half:], "mass", behind), "mass", behind)
    opposite = jnp.concatenate([first, second], axis=0)
    stacked = jnp.stack([pieces[me], from_behind, opposite, from_ahead])
    return stacked[(me - jnp.arange(mass_count)) % mass_count]


def shards(spectra, window, cluster):
    s_dev, num_bins = spectra.shape
    mass_count = lax.axis_size("mass")
    tile_count = lax.axis_size("tile")
    per_window = CL_DEV * tile_count
    capacity = 2 * s_dev // mass_count
    slot_count = mass_count * capacity
    values = spectra.astype(jnp.float32)
    scaled = (values * lax.rsqrt(jnp.mean(values * values, axis=1, keepdims=True) + 1e-06)).astype(
        jnp.bfloat16
    )
    target = window[:, 0]
    global_ids = target * per_window + cluster
    member = (target[:, None] == jnp.arange(mass_count, dtype=jnp.int32)[None, :]).astype(jnp.int32)
    before = jnp.cumsum(member, axis=0) - member
    slot_rank = jnp.sum(before * member, axis=1)
    position = target * capacity + slot_rank
    chosen = jnp.arange(slot_count, dtype=jnp.int32)[:, None] == position[None, :]
    outgoing = jnp.dot(
        chosen.astype(jnp.bfloat16), scaled, preferred_element_type=jnp.float32
    ).astype(jnp.bfloat16)
    outgoing = outgoing.reshape(mass_count, capacity, num_bins)
    labels = jnp.max(jnp.where(chosen, global_ids[None, :], -1), axis=1).reshape(
        mass_count, capacity
    )
    arrived = exchange_over_mass(outgoing, mass_count)
    arrived_labels = exchange_over_mass(labels, mass_count)
    arrived = arrived.reshape(slot_count, num_bins)
    arrived_labels = arrived_labels.reshape(slot_count)
    gathered = lax.all_gather(arrived, "tile", axis=0, tiled=True)
    gathered_labels = lax.all_gather(arrived_labels, "tile", axis=0, tiled=True)
    tile = lax.axis_index("tile")
    swap = [(i, i ^ 1) for i in range(tile_count)]
    half = tile % 2
    partner_rows = lax.ppermute(arrived, "tile", swap)
    pair_rows = jnp.concatenate([arrived, partner_rows], axis=0)
    owners = jnp.where(jnp.arange(2 * CL_DEV) < CL_DEV, tile, tile ^ 1)
    own_ids = (
        lax.axis_index("mass") * per_window
        + owners * CL_DEV
        + jnp.arange(2 * CL_DEV, dtype=jnp.int32) % CL_DEV
    )
    one_hot = (own_ids[:, None] == gathered_labels[None, :]).astype(jnp.bfloat16)
    parts = 2
    mine = jnp.zeros((slot_count, gathered.shape[0]), jnp.float32)
    other = (1 - half) * (gathered.shape[0] // 2)
    returned = []
    sums = None
    for part in range(parts):
        mine, theirs, part_sums = gram_consensus(
            half.reshape(1), part, parts, pair_rows, one_hot, gathered, mine
        )
        returned.append((part * theirs.shape[1], lax.ppermute(theirs, "tile", swap)))
        sums = part_sums if sums is None else sums + part_sums
    gram_tiles = mine
    for offset, piece in returned:
        gram_tiles = lax.dynamic_update_slice(gram_tiles, piece, (0, other + offset))
    consensus = sums[:CL_DEV] + lax.ppermute(sums[CL_DEV:], "tile", swap)
    return (gram_tiles, consensus)


def solution(mesh):
    in_specs = (P(("mass", "tile"), None), P(("mass", "tile"), None), P(("mass", "tile")))
    out_specs = (P(("mass", "tile"), None), P(("mass", "tile"), None))
    return jax.shard_map(shards, mesh=mesh, in_specs=in_specs, out_specs=out_specs, check_vma=False)
```

```python
import functools

import jax
import jax.numpy as jnp
from jax import lax
from jax.experimental import pallas as pl
from jax.experimental.pallas import tpu as pltpu
from jax.sharding import PartitionSpec as P

CL_DEV = 4

def _gram_consensus_kernel(scale, rows, half_ref, a_ref, oh_ref, p_ref, mine_ref, theirs_ref, c_ref):
    j = pl.program_id(0)
    blk = p_ref[...]
    res = lax.dot_general(
        a_ref[...], blk, (((1,), (1,)), ((), ())), preferred_element_type=jnp.float32
    ) * scale
    mine_ref[...] = res[:rows]
    theirs_ref[...] = res[rows:]

    @pl.when(j == 0)
    def _():
        c_ref[...] = jnp.zeros_like(c_ref)

    c_ref[...] += jnp.dot(oh_ref[...], blk, preferred_element_type=jnp.float32)


def gram_consensus(half, pair_rows, one_hot, gathered, block_rows=1024):
    rows = pair_rows.shape[0] // 2
    bins = pair_rows.shape[1]
    total = gathered.shape[0]
    heads = one_hot.shape[0]
    steps = total // 2 // block_rows
    flops = 2 * 2 * rows * (total // 2) * bins + 2 * heads * (total // 2) * bins
    bytes_accessed = 2 * (2 * rows * bins + heads * total // 2 + total // 2 * bins) + 4 * (
        2 * rows * total // 2 + heads * bins
    )
    grid_spec = pltpu.PrefetchScalarGridSpec(
        num_scalar_prefetch=1,
        grid=(steps,),
        in_specs=[
            pl.BlockSpec((2 * rows, bins), lambda j, h: (0, 0)),
            pl.BlockSpec((heads, block_rows), lambda j, h: (0, h[0] * steps + j)),
            pl.BlockSpec((block_rows, bins), lambda j, h: (h[0] * steps + j, 0)),
        ],
        out_specs=[
            pl.BlockSpec((rows, block_rows), lambda j, h: (0, h[0] * steps + j)),
            pl.BlockSpec((rows, block_rows), lambda j, h: (0, j)),
            pl.BlockSpec((heads, bins), lambda j, h: (0, 0)),
        ],
    )
    return pl.pallas_call(
        functools.partial(_gram_consensus_kernel, 1.0 / bins, rows),
        grid_spec=grid_spec,
        out_shape=[
            jax.ShapeDtypeStruct((rows, total), jnp.float32),
            jax.ShapeDtypeStruct((rows, total // 2), jnp.float32),
            jax.ShapeDtypeStruct((heads, bins), jnp.float32),
        ],
        compiler_params=pltpu.CompilerParams(dimension_semantics=("arbitrary",)),
        cost_estimate=pl.CostEstimate(flops=flops, bytes_accessed=bytes_accessed, transcendentals=0),
    )(half, pair_rows, one_hot, gathered)


def exchange_over_mass(pieces, mass_count):
    me = lax.axis_index("mass")
    ahead = [(i, (i + 1) % mass_count) for i in range(mass_count)]
    behind = [(i, (i - 1) % mass_count) for i in range(mass_count)]
    from_behind = lax.ppermute(pieces[(me + 1) % mass_count], "mass", ahead)
    from_ahead = lax.ppermute(pieces[(me - 1) % mass_count], "mass", behind)
    far = pieces[(me + 2) % mass_count]
    half = far.shape[0] // 2
    first = lax.ppermute(lax.ppermute(far[:half], "mass", ahead), "mass", ahead)
    second = lax.ppermute(lax.ppermute(far[half:], "mass", behind), "mass", behind)
    opposite = jnp.concatenate([first, second], axis=0)
    stacked = jnp.stack([pieces[me], from_behind, opposite, from_ahead])
    return stacked[(me - jnp.arange(mass_count)) % mass_count]


def shards(spectra, window, cluster):
    s_dev, num_bins = spectra.shape
    mass_count = lax.axis_size("mass")
    tile_count = lax.axis_size("tile")
    per_window = CL_DEV * tile_count
    capacity = 2 * s_dev // mass_count
    slot_count = mass_count * capacity
    values = spectra.astype(jnp.float32)
    scaled = (values * lax.rsqrt(jnp.mean(values * values, axis=1, keepdims=True) + 1e-06)).astype(
        jnp.bfloat16
    )
    target = window[:, 0]
    global_ids = target * per_window + cluster
    member = (target[:, None] == jnp.arange(mass_count, dtype=jnp.int32)[None, :]).astype(jnp.int32)
    before = jnp.cumsum(member, axis=0) - member
    slot_rank = jnp.sum(before * member, axis=1)
    position = target * capacity + slot_rank
    chosen = jnp.arange(slot_count, dtype=jnp.int32)[:, None] == position[None, :]
    outgoing = jnp.dot(
        chosen.astype(jnp.bfloat16), scaled, preferred_element_type=jnp.float32
    ).astype(jnp.bfloat16)
    outgoing = outgoing.reshape(mass_count, capacity, num_bins)
    labels = jnp.max(jnp.where(chosen, global_ids[None, :], -1), axis=1).reshape(
        mass_count, capacity
    )
    arrived = exchange_over_mass(outgoing, mass_count)
    arrived_labels = exchange_over_mass(labels, mass_count)
    arrived = arrived.reshape(slot_count, num_bins)
    arrived_labels = arrived_labels.reshape(slot_count)
    gathered = lax.all_gather(arrived, "tile", axis=0, tiled=True)
    gathered_labels = lax.all_gather(arrived_labels, "tile", axis=0, tiled=True)
    tile = lax.axis_index("tile")
    swap = [(i, i ^ 1) for i in range(tile_count)]
    half = tile % 2
    partner_rows = lax.ppermute(arrived, "tile", swap)
    pair_rows = jnp.concatenate([arrived, partner_rows], axis=0)
    owners = jnp.where(jnp.arange(2 * CL_DEV) < CL_DEV, tile, tile ^ 1)
    own_ids = (
        lax.axis_index("mass") * per_window
        + owners * CL_DEV
        + jnp.arange(2 * CL_DEV, dtype=jnp.int32) % CL_DEV
    )
    one_hot = (own_ids[:, None] == gathered_labels[None, :]).astype(jnp.bfloat16)
    mine, theirs, sums = gram_consensus(half.reshape(1), pair_rows, one_hot, gathered)
    pieces = 4
    step = theirs.shape[0] // pieces
    gram_tiles = mine
    for p in range(pieces):
        returned = lax.ppermute(theirs[p * step:(p + 1) * step], "tile", swap)
        gram_tiles = lax.dynamic_update_slice(
            gram_tiles, returned, (p * step, (1 - half) * theirs.shape[1])
        )
    consensus = sums[:CL_DEV] + lax.ppermute(sums[CL_DEV:], "tile", swap)
    return (gram_tiles, consensus)


def solution(mesh):
    in_specs = (P(("mass", "tile"), None), P(("mass", "tile"), None), P(("mass", "tile")))
    out_specs = (P(("mass", "tile"), None), P(("mass", "tile"), None))
    return jax.shard_map(shards, mesh=mesh, in_specs=in_specs, out_specs=out_specs, check_vma=False)
```

```python
import functools

import jax
import jax.numpy as jnp
from jax import lax
from jax.experimental import pallas as pl
from jax.experimental.pallas import tpu as pltpu
from jax.sharding import PartitionSpec as P

CL_DEV = 4

def _gram_consensus_kernel(scale, rows, pieces, half_ref, a_ref, oh_ref, p_ref, mine_ref, *out_refs):
    theirs_refs, c_mine_ref, c_theirs_ref = out_refs[:pieces], out_refs[pieces], out_refs[pieces + 1]
    j = pl.program_id(0)
    blk = p_ref[...]
    res = lax.dot_general(
        a_ref[...], blk, (((1,), (1,)), ((), ())), preferred_element_type=jnp.float32
    ) * scale
    mine_ref[...] = res[:rows]
    step = rows // pieces
    for p, ref in enumerate(theirs_refs):
        ref[...] = res[rows + p * step:rows + (p + 1) * step]

    @pl.when(j == 0)
    def _():
        c_mine_ref[...] = jnp.zeros_like(c_mine_ref)
        c_theirs_ref[...] = jnp.zeros_like(c_theirs_ref)

    sums = jnp.dot(oh_ref[...], blk, preferred_element_type=jnp.float32)
    heads = sums.shape[0] // 2
    c_mine_ref[...] += sums[:heads]
    c_theirs_ref[...] += sums[heads:]


def gram_consensus(half, pair_rows, one_hot, gathered, pieces=4, block_rows=1024):
    rows = pair_rows.shape[0] // 2
    bins = pair_rows.shape[1]
    total = gathered.shape[0]
    heads = one_hot.shape[0]
    steps = total // 2 // block_rows
    step = rows // pieces
    flops = 2 * 2 * rows * (total // 2) * bins + 2 * heads * (total // 2) * bins
    bytes_accessed = 2 * (2 * rows * bins + heads * total // 2 + total // 2 * bins) + 4 * (
        2 * rows * total // 2 + heads * bins
    )
    grid_spec = pltpu.PrefetchScalarGridSpec(
        num_scalar_prefetch=1,
        grid=(steps,),
        in_specs=[
            pl.BlockSpec((2 * rows, bins), lambda j, h: (0, 0)),
            pl.BlockSpec((heads, block_rows), lambda j, h: (0, h[0] * steps + j)),
            pl.BlockSpec((block_rows, bins), lambda j, h: (h[0] * steps + j, 0)),
        ],
        out_specs=[pl.BlockSpec((rows, block_rows), lambda j, h: (0, h[0] * steps + j))]
        + [pl.BlockSpec((step, block_rows), lambda j, h: (0, j)) for _ in range(pieces)]
        + [pl.BlockSpec((heads // 2, bins), lambda j, h: (0, 0))] * 2,
    )
    return pl.pallas_call(
        functools.partial(_gram_consensus_kernel, 1.0 / bins, rows, pieces),
        grid_spec=grid_spec,
        out_shape=[jax.ShapeDtypeStruct((rows, total), jnp.float32)]
        + [jax.ShapeDtypeStruct((step, total // 2), jnp.float32) for _ in range(pieces)]
        + [jax.ShapeDtypeStruct((heads // 2, bins), jnp.float32)] * 2,
        compiler_params=pltpu.CompilerParams(dimension_semantics=("arbitrary",)),
        cost_estimate=pl.CostEstimate(flops=flops, bytes_accessed=bytes_accessed, transcendentals=0),
    )(half, pair_rows, one_hot, gathered)


def exchange_over_mass(pieces, mass_count):
    me = lax.axis_index("mass")
    ahead = [(i, (i + 1) % mass_count) for i in range(mass_count)]
    behind = [(i, (i - 1) % mass_count) for i in range(mass_count)]
    from_behind = lax.ppermute(pieces[(me + 1) % mass_count], "mass", ahead)
    from_ahead = lax.ppermute(pieces[(me - 1) % mass_count], "mass", behind)
    far = pieces[(me + 2) % mass_count]
    half = far.shape[0] // 2
    first = lax.ppermute(lax.ppermute(far[:half], "mass", ahead), "mass", ahead)
    second = lax.ppermute(lax.ppermute(far[half:], "mass", behind), "mass", behind)
    opposite = jnp.concatenate([first, second], axis=0)
    stacked = jnp.stack([pieces[me], from_behind, opposite, from_ahead])
    return stacked[(me - jnp.arange(mass_count)) % mass_count]


def shards(spectra, window, cluster):
    s_dev, num_bins = spectra.shape
    mass_count = lax.axis_size("mass")
    tile_count = lax.axis_size("tile")
    per_window = CL_DEV * tile_count
    capacity = 2 * s_dev // mass_count
    slot_count = mass_count * capacity
    values = spectra.astype(jnp.float32)
    scaled = (values * lax.rsqrt(jnp.mean(values * values, axis=1, keepdims=True) + 1e-06)).astype(
        jnp.bfloat16
    )
    target = window[:, 0]
    global_ids = target * per_window + cluster
    member = (target[:, None] == jnp.arange(mass_count, dtype=jnp.int32)[None, :]).astype(jnp.int32)
    before = jnp.cumsum(member, axis=0) - member
    slot_rank = jnp.sum(before * member, axis=1)
    position = target * capacity + slot_rank
    chosen = jnp.arange(slot_count, dtype=jnp.int32)[:, None] == position[None, :]
    outgoing = jnp.dot(
        chosen.astype(jnp.bfloat16), scaled, preferred_element_type=jnp.float32
    ).astype(jnp.bfloat16)
    outgoing = outgoing.reshape(mass_count, capacity, num_bins)
    labels = jnp.max(jnp.where(chosen, global_ids[None, :], -1), axis=1).reshape(
        mass_count, capacity
    )
    arrived = exchange_over_mass(outgoing, mass_count)
    arrived_labels = exchange_over_mass(labels, mass_count)
    arrived = arrived.reshape(slot_count, num_bins)
    arrived_labels = arrived_labels.reshape(slot_count)
    gathered = lax.all_gather(arrived, "tile", axis=0, tiled=True)
    gathered_labels = lax.all_gather(arrived_labels, "tile", axis=0, tiled=True)
    tile = lax.axis_index("tile")
    swap = [(i, i ^ 1) for i in range(tile_count)]
    half = tile % 2
    partner_rows = lax.ppermute(arrived, "tile", swap)
    pair_rows = jnp.concatenate([arrived, partner_rows], axis=0)
    owners = jnp.where(jnp.arange(2 * CL_DEV) < CL_DEV, tile, tile ^ 1)
    own_ids = (
        lax.axis_index("mass") * per_window
        + owners * CL_DEV
        + jnp.arange(2 * CL_DEV, dtype=jnp.int32) % CL_DEV
    )
    one_hot = (own_ids[:, None] == gathered_labels[None, :]).astype(jnp.bfloat16)
    outs = gram_consensus(half.reshape(1), pair_rows, one_hot, gathered)
    gram_tiles, theirs, sums_mine, sums_theirs = outs[0], outs[1:-2], outs[-2], outs[-1]
    other = (1 - half) * (gathered.shape[0] // 2)
    for p, piece in enumerate(theirs):
        returned = lax.ppermute(piece, "tile", swap)
        gram_tiles = lax.dynamic_update_slice(gram_tiles, returned, (p * piece.shape[0], other))
    consensus = sums_mine + lax.ppermute(sums_theirs, "tile", swap)
    return (gram_tiles, consensus)


def solution(mesh):
    in_specs = (P(("mass", "tile"), None), P(("mass", "tile"), None), P(("mass", "tile")))
    out_specs = (P(("mass", "tile"), None), P(("mass", "tile"), None))
    return jax.shard_map(shards, mesh=mesh, in_specs=in_specs, out_specs=out_specs, check_vma=False)
```

```python
import functools

import jax
import jax.numpy as jnp
from jax import lax
from jax.experimental import pallas as pl
from jax.experimental.pallas import tpu as pltpu
from jax.sharding import PartitionSpec as P

CL_DEV = 4

def _gram_consensus_kernel(scale, rows, pieces, half_ref, a_ref, oh_ref, p_ref, mine_ref, *out_refs):
    theirs_refs, c_mine_ref, c_theirs_ref = out_refs[:pieces], out_refs[pieces], out_refs[pieces + 1]
    j = pl.program_id(0)
    blk = p_ref[...]
    res = lax.dot_general(
        a_ref[...], blk, (((1,), (1,)), ((), ())), preferred_element_type=jnp.float32
    ) * scale
    mine_ref[...] = res[:rows]
    step = rows // pieces
    for p, ref in enumerate(theirs_refs):
        ref[...] = res[rows + p * step:rows + (p + 1) * step]

    @pl.when(j == 0)
    def _():
        c_mine_ref[...] = jnp.zeros_like(c_mine_ref)
        c_theirs_ref[...] = jnp.zeros_like(c_theirs_ref)

    sums = jnp.dot(oh_ref[...], blk, preferred_element_type=jnp.float32)
    heads = sums.shape[0] // 2
    c_mine_ref[...] += sums[:heads]
    c_theirs_ref[...] += sums[heads:]


def gram_consensus(half, pair_rows, one_hot, gathered, pieces=4, block_rows=1024):
    rows = pair_rows.shape[0] // 2
    bins = pair_rows.shape[1]
    total = gathered.shape[0]
    heads = one_hot.shape[0]
    steps = total // 2 // block_rows
    step = rows // pieces
    flops = 2 * 2 * rows * (total // 2) * bins + 2 * heads * (total // 2) * bins
    bytes_accessed = 2 * (2 * rows * bins + heads * total // 2 + total // 2 * bins) + 4 * (
        2 * rows * total // 2 + heads * bins
    )
    grid_spec = pltpu.PrefetchScalarGridSpec(
        num_scalar_prefetch=1,
        grid=(steps,),
        in_specs=[
            pl.BlockSpec((2 * rows, bins), lambda j, h: (0, 0)),
            pl.BlockSpec((heads, block_rows), lambda j, h: (0, h[0] * steps + j)),
            pl.BlockSpec((block_rows, bins), lambda j, h: (h[0] * steps + j, 0)),
        ],
        out_specs=[pl.BlockSpec((rows, block_rows), lambda j, h: (0, h[0] * steps + j))]
        + [pl.BlockSpec((step, block_rows), lambda j, h: (0, j)) for _ in range(pieces)]
        + [pl.BlockSpec((heads // 2, bins), lambda j, h: (0, 0))] * 2,
    )
    return pl.pallas_call(
        functools.partial(_gram_consensus_kernel, 1.0 / bins, rows, pieces),
        grid_spec=grid_spec,
        out_shape=[jax.ShapeDtypeStruct((rows, total), jnp.float32)]
        + [jax.ShapeDtypeStruct((step, total // 2), jnp.float32) for _ in range(pieces)]
        + [jax.ShapeDtypeStruct((heads // 2, bins), jnp.float32)] * 2,
        compiler_params=pltpu.CompilerParams(dimension_semantics=("arbitrary",)),
        cost_estimate=pl.CostEstimate(flops=flops, bytes_accessed=bytes_accessed, transcendentals=0),
    )(half, pair_rows, one_hot, gathered)


def exchange_over_mass(pieces, mass_count):
    me = lax.axis_index("mass")
    ahead = [(i, (i + 1) % mass_count) for i in range(mass_count)]
    behind = [(i, (i - 1) % mass_count) for i in range(mass_count)]
    far = pieces[(me + 2) % mass_count]
    size, half = far.shape[0], far.shape[0] // 2
    went_ahead = lax.ppermute(
        jnp.concatenate([pieces[(me + 1) % mass_count], far[:half]]), "mass", ahead
    )
    went_behind = lax.ppermute(
        jnp.concatenate([pieces[(me - 1) % mass_count], far[half:]]), "mass", behind
    )
    first = lax.ppermute(went_ahead[size:], "mass", ahead)
    second = lax.ppermute(went_behind[size:], "mass", behind)
    opposite = jnp.concatenate([first, second], axis=0)
    stacked = jnp.stack([pieces[me], went_ahead[:size], opposite, went_behind[:size]])
    return stacked[(me - jnp.arange(mass_count)) % mass_count]


def shards(spectra, window, cluster):
    s_dev, num_bins = spectra.shape
    mass_count = lax.axis_size("mass")
    tile_count = lax.axis_size("tile")
    per_window = CL_DEV * tile_count
    capacity = 2 * s_dev // mass_count
    slot_count = mass_count * capacity
    values = spectra.astype(jnp.float32)
    scaled = (values * lax.rsqrt(jnp.mean(values * values, axis=1, keepdims=True) + 1e-06)).astype(
        jnp.bfloat16
    )
    target = window[:, 0]
    global_ids = target * per_window + cluster
    member = (target[:, None] == jnp.arange(mass_count, dtype=jnp.int32)[None, :]).astype(jnp.int32)
    before = jnp.cumsum(member, axis=0) - member
    slot_rank = jnp.sum(before * member, axis=1)
    position = target * capacity + slot_rank
    chosen = jnp.arange(slot_count, dtype=jnp.int32)[:, None] == position[None, :]
    outgoing = jnp.dot(
        chosen.astype(jnp.bfloat16), scaled, preferred_element_type=jnp.float32
    ).astype(jnp.bfloat16)
    outgoing = outgoing.reshape(mass_count, capacity, num_bins)
    labels = jnp.max(jnp.where(chosen, global_ids[None, :], -1), axis=1).reshape(
        mass_count, capacity
    )
    arrived = exchange_over_mass(outgoing, mass_count)
    arrived_labels = exchange_over_mass(labels, mass_count)
    arrived = arrived.reshape(slot_count, num_bins)
    arrived_labels = arrived_labels.reshape(slot_count)
    gathered = lax.all_gather(arrived, "tile", axis=0, tiled=True)
    gathered_labels = lax.all_gather(arrived_labels, "tile", axis=0, tiled=True)
    tile = lax.axis_index("tile")
    swap = [(i, i ^ 1) for i in range(tile_count)]
    half = tile % 2
    partner_rows = lax.ppermute(arrived, "tile", swap)
    pair_rows = jnp.concatenate([arrived, partner_rows], axis=0)
    owners = jnp.where(jnp.arange(2 * CL_DEV) < CL_DEV, tile, tile ^ 1)
    own_ids = (
        lax.axis_index("mass") * per_window
        + owners * CL_DEV
        + jnp.arange(2 * CL_DEV, dtype=jnp.int32) % CL_DEV
    )
    one_hot = (own_ids[:, None] == gathered_labels[None, :]).astype(jnp.bfloat16)
    outs = gram_consensus(half.reshape(1), pair_rows, one_hot, gathered)
    gram_tiles, theirs, sums_mine, sums_theirs = outs[0], outs[1:-2], outs[-2], outs[-1]
    other = (1 - half) * (gathered.shape[0] // 2)
    for p, piece in enumerate(theirs):
        returned = lax.ppermute(piece, "tile", swap)
        gram_tiles = lax.dynamic_update_slice(gram_tiles, returned, (p * piece.shape[0], other))
    consensus = sums_mine + lax.ppermute(sums_theirs, "tile", swap)
    return (gram_tiles, consensus)


def solution(mesh):
    in_specs = (P(("mass", "tile"), None), P(("mass", "tile"), None), P(("mass", "tile")))
    out_specs = (P(("mass", "tile"), None), P(("mass", "tile"), None))
    return jax.shard_map(shards, mesh=mesh, in_specs=in_specs, out_specs=out_specs, check_vma=False)
```

```python
import functools

import jax
import jax.numpy as jnp
from jax import lax
from jax.experimental import pallas as pl
from jax.experimental.pallas import tpu as pltpu
from jax.sharding import PartitionSpec as P

CL_DEV = 4

def _gram_consensus_kernel(scale, rows, pieces, half_ref, a_ref, oh_ref, p_ref, mine_ref, *out_refs):
    theirs_refs, c_mine_ref, c_theirs_ref = out_refs[:pieces], out_refs[pieces], out_refs[pieces + 1]
    j = pl.program_id(0)
    blk = p_ref[...]
    res = lax.dot_general(
        a_ref[...], blk, (((1,), (1,)), ((), ())), preferred_element_type=jnp.float32
    ) * scale
    mine_ref[...] = res[:rows]
    step = rows // pieces
    for p, ref in enumerate(theirs_refs):
        ref[...] = res[rows + p * step:rows + (p + 1) * step]

    @pl.when(j == 0)
    def _():
        c_mine_ref[...] = jnp.zeros_like(c_mine_ref)
        c_theirs_ref[...] = jnp.zeros_like(c_theirs_ref)

    sums = jnp.dot(oh_ref[...], blk, preferred_element_type=jnp.float32)
    heads = sums.shape[0] // 2
    c_mine_ref[...] += sums[:heads]
    c_theirs_ref[...] += sums[heads:]


def gram_consensus(half, pair_rows, one_hot, gathered, pieces=2, block_rows=1024):
    rows = pair_rows.shape[0] // 2
    bins = pair_rows.shape[1]
    total = gathered.shape[0]
    heads = one_hot.shape[0]
    steps = total // 2 // block_rows
    step = rows // pieces
    flops = 2 * 2 * rows * (total // 2) * bins + 2 * heads * (total // 2) * bins
    bytes_accessed = 2 * (2 * rows * bins + heads * total // 2 + total // 2 * bins) + 4 * (
        2 * rows * total // 2 + heads * bins
    )
    grid_spec = pltpu.PrefetchScalarGridSpec(
        num_scalar_prefetch=1,
        grid=(steps,),
        in_specs=[
            pl.BlockSpec((2 * rows, bins), lambda j, h: (0, 0)),
            pl.BlockSpec((heads, block_rows), lambda j, h: (0, h[0] * steps + j)),
            pl.BlockSpec((block_rows, bins), lambda j, h: (h[0] * steps + j, 0)),
        ],
        out_specs=[pl.BlockSpec((rows, block_rows), lambda j, h: (0, h[0] * steps + j))]
        + [pl.BlockSpec((step, block_rows), lambda j, h: (0, j)) for _ in range(pieces)]
        + [pl.BlockSpec((heads // 2, bins), lambda j, h: (0, 0))] * 2,
    )
    return pl.pallas_call(
        functools.partial(_gram_consensus_kernel, 1.0 / bins, rows, pieces),
        grid_spec=grid_spec,
        out_shape=[jax.ShapeDtypeStruct((rows, total), jnp.float32)]
        + [jax.ShapeDtypeStruct((step, total // 2), jnp.float32) for _ in range(pieces)]
        + [jax.ShapeDtypeStruct((heads // 2, bins), jnp.float32)] * 2,
        compiler_params=pltpu.CompilerParams(dimension_semantics=("arbitrary",)),
        cost_estimate=pl.CostEstimate(flops=flops, bytes_accessed=bytes_accessed, transcendentals=0),
    )(half, pair_rows, one_hot, gathered)


def exchange_over_mass(pieces, mass_count):
    me = lax.axis_index("mass")
    ahead = [(i, (i + 1) % mass_count) for i in range(mass_count)]
    behind = [(i, (i - 1) % mass_count) for i in range(mass_count)]
    from_behind = lax.ppermute(pieces[(me + 1) % mass_count], "mass", ahead)
    from_ahead = lax.ppermute(pieces[(me - 1) % mass_count], "mass", behind)
    far = pieces[(me + 2) % mass_count]
    half = far.shape[0] // 2
    first = lax.ppermute(lax.ppermute(far[:half], "mass", ahead), "mass", ahead)
    second = lax.ppermute(lax.ppermute(far[half:], "mass", behind), "mass", behind)
    opposite = jnp.concatenate([first, second], axis=0)
    stacked = jnp.stack([pieces[me], from_behind, opposite, from_ahead])
    return stacked[(me - jnp.arange(mass_count)) % mass_count]


def shards(spectra, window, cluster):
    s_dev, num_bins = spectra.shape
    mass_count = lax.axis_size("mass")
    tile_count = lax.axis_size("tile")
    per_window = CL_DEV * tile_count
    capacity = 2 * s_dev // mass_count
    slot_count = mass_count * capacity
    values = spectra.astype(jnp.float32)
    scaled = (values * lax.rsqrt(jnp.mean(values * values, axis=1, keepdims=True) + 1e-06)).astype(
        jnp.bfloat16
    )
    target = window[:, 0]
    global_ids = target * per_window + cluster
    member = (target[:, None] == jnp.arange(mass_count, dtype=jnp.int32)[None, :]).astype(jnp.int32)
    before = jnp.cumsum(member, axis=0) - member
    slot_rank = jnp.sum(before * member, axis=1)
    position = target * capacity + slot_rank
    chosen = jnp.arange(slot_count, dtype=jnp.int32)[:, None] == position[None, :]
    outgoing = jnp.dot(
        chosen.astype(jnp.bfloat16), scaled, preferred_element_type=jnp.float32
    ).astype(jnp.bfloat16)
    outgoing = outgoing.reshape(mass_count, capacity, num_bins)
    labels = jnp.max(jnp.where(chosen, global_ids[None, :], -1), axis=1).reshape(
        mass_count, capacity
    )
    arrived = exchange_over_mass(outgoing, mass_count)
    arrived_labels = exchange_over_mass(labels, mass_count)
    arrived = arrived.reshape(slot_count, num_bins)
    arrived_labels = arrived_labels.reshape(slot_count)
    gathered = lax.all_gather(arrived, "tile", axis=0, tiled=True)
    gathered_labels = lax.all_gather(arrived_labels, "tile", axis=0, tiled=True)
    tile = lax.axis_index("tile")
    swap = [(i, i ^ 1) for i in range(tile_count)]
    half = tile % 2
    partner_rows = lax.ppermute(arrived, "tile", swap)
    pair_rows = jnp.concatenate([arrived, partner_rows], axis=0)
    owners = jnp.where(jnp.arange(2 * CL_DEV) < CL_DEV, tile, tile ^ 1)
    own_ids = (
        lax.axis_index("mass") * per_window
        + owners * CL_DEV
        + jnp.arange(2 * CL_DEV, dtype=jnp.int32) % CL_DEV
    )
    one_hot = (own_ids[:, None] == gathered_labels[None, :]).astype(jnp.bfloat16)
    outs = gram_consensus(half.reshape(1), pair_rows, one_hot, gathered)
    gram_tiles, theirs, sums_mine, sums_theirs = outs[0], outs[1:-2], outs[-2], outs[-1]
    other = (1 - half) * (gathered.shape[0] // 2)
    for p, piece in enumerate(theirs):
        returned = lax.ppermute(piece, "tile", swap)
        gram_tiles = lax.dynamic_update_slice(gram_tiles, returned, (p * piece.shape[0], other))
    consensus = sums_mine + lax.ppermute(sums_theirs, "tile", swap)
    return (gram_tiles, consensus)


def solution(mesh):
    in_specs = (P(("mass", "tile"), None), P(("mass", "tile"), None), P(("mass", "tile")))
    out_specs = (P(("mass", "tile"), None), P(("mass", "tile"), None))
    return jax.shard_map(shards, mesh=mesh, in_specs=in_specs, out_specs=out_specs, check_vma=False)
```

```python
import functools

import jax
import jax.numpy as jnp
from jax import lax
from jax.experimental import pallas as pl
from jax.experimental.pallas import tpu as pltpu
from jax.sharding import PartitionSpec as P

CL_DEV = 4

def _gram_consensus_kernel(scale, rows, pieces, half_ref, a_ref, oh_ref, p_ref, mine_ref, *out_refs):
    theirs_refs, c_mine_ref, c_theirs_ref = out_refs[:pieces], out_refs[pieces], out_refs[pieces + 1]
    j = pl.program_id(0)
    blk = p_ref[...]
    res = lax.dot_general(
        a_ref[...], blk, (((1,), (1,)), ((), ())), preferred_element_type=jnp.float32
    ) * scale
    mine_ref[...] = res[:rows]
    step = rows // pieces
    for p, ref in enumerate(theirs_refs):
        ref[...] = res[rows + p * step:rows + (p + 1) * step]

    @pl.when(j == 0)
    def _():
        c_mine_ref[...] = jnp.zeros_like(c_mine_ref)
        c_theirs_ref[...] = jnp.zeros_like(c_theirs_ref)

    sums = jnp.dot(oh_ref[...], blk, preferred_element_type=jnp.float32)
    heads = sums.shape[0] // 2
    c_mine_ref[...] += sums[:heads]
    c_theirs_ref[...] += sums[heads:]


def gram_consensus(half, pair_rows, one_hot, gathered, pieces=4, block_rows=1024):
    rows = pair_rows.shape[0] // 2
    bins = pair_rows.shape[1]
    total = gathered.shape[0]
    heads = one_hot.shape[0]
    steps = total // 2 // block_rows
    step = rows // pieces
    flops = 2 * 2 * rows * (total // 2) * bins + 2 * heads * (total // 2) * bins
    bytes_accessed = 2 * (2 * rows * bins + heads * total // 2 + total // 2 * bins) + 4 * (
        2 * rows * total // 2 + heads * bins
    )
    grid_spec = pltpu.PrefetchScalarGridSpec(
        num_scalar_prefetch=1,
        grid=(steps,),
        in_specs=[
            pl.BlockSpec((2 * rows, bins), lambda j, h: (0, 0)),
            pl.BlockSpec((heads, block_rows), lambda j, h: (0, h[0] * steps + j)),
            pl.BlockSpec((block_rows, bins), lambda j, h: (h[0] * steps + j, 0)),
        ],
        out_specs=[pl.BlockSpec((rows, block_rows), lambda j, h: (0, h[0] * steps + j))]
        + [pl.BlockSpec((step, block_rows), lambda j, h: (0, j)) for _ in range(pieces)]
        + [pl.BlockSpec((heads // 2, bins), lambda j, h: (0, 0))] * 2,
    )
    return pl.pallas_call(
        functools.partial(_gram_consensus_kernel, 1.0 / bins, rows, pieces),
        grid_spec=grid_spec,
        out_shape=[jax.ShapeDtypeStruct((rows, total), jnp.float32)]
        + [jax.ShapeDtypeStruct((step, total // 2), jnp.float32) for _ in range(pieces)]
        + [jax.ShapeDtypeStruct((heads // 2, bins), jnp.float32)] * 2,
        compiler_params=pltpu.CompilerParams(dimension_semantics=("arbitrary",)),
        cost_estimate=pl.CostEstimate(flops=flops, bytes_accessed=bytes_accessed, transcendentals=0),
    )(half, pair_rows, one_hot, gathered)


def exchange_over_mass(pieces, mass_count):
    me = lax.axis_index("mass")
    ahead = [(i, (i + 1) % mass_count) for i in range(mass_count)]
    behind = [(i, (i - 1) % mass_count) for i in range(mass_count)]
    from_behind = lax.ppermute(pieces[(me + 1) % mass_count], "mass", ahead)
    from_ahead = lax.ppermute(pieces[(me - 1) % mass_count], "mass", behind)
    far = pieces[(me + 2) % mass_count]
    half = far.shape[0] // 2
    first = lax.ppermute(lax.ppermute(far[:half], "mass", ahead), "mass", ahead)
    second = lax.ppermute(lax.ppermute(far[half:], "mass", behind), "mass", behind)
    opposite = jnp.concatenate([first, second], axis=0)
    stacked = jnp.stack([pieces[me], from_behind, opposite, from_ahead])
    return stacked[(me - jnp.arange(mass_count)) % mass_count]


def shards(spectra, window, cluster):
    s_dev, num_bins = spectra.shape
    mass_count = lax.axis_size("mass")
    tile_count = lax.axis_size("tile")
    per_window = CL_DEV * tile_count
    capacity = 2 * s_dev // mass_count
    slot_count = mass_count * capacity
    values = spectra.astype(jnp.float32)
    scaled = (values * lax.rsqrt(jnp.mean(values * values, axis=1, keepdims=True) + 1e-06)).astype(
        jnp.bfloat16
    )
    target = window[:, 0]
    global_ids = target * per_window + cluster
    member = (target[:, None] == jnp.arange(mass_count, dtype=jnp.int32)[None, :]).astype(jnp.int32)
    before = jnp.cumsum(member, axis=0) - member
    slot_rank = jnp.sum(before * member, axis=1)
    position = target * capacity + slot_rank
    chosen = jnp.arange(slot_count, dtype=jnp.int32)[:, None] == position[None, :]
    outgoing = jnp.dot(
        chosen.astype(jnp.bfloat16), scaled, preferred_element_type=jnp.float32
    ).astype(jnp.bfloat16)
    outgoing = outgoing.reshape(mass_count, capacity, num_bins)
    labels = jnp.max(jnp.where(chosen, global_ids[None, :], -1), axis=1).reshape(
        mass_count, capacity
    )
    arrived = exchange_over_mass(outgoing, mass_count)
    arrived_labels = exchange_over_mass(labels, mass_count)
    arrived = arrived.reshape(slot_count, num_bins)
    arrived_labels = arrived_labels.reshape(slot_count)
    gathered = lax.all_gather(arrived, "tile", axis=0, tiled=True)
    gathered_labels = lax.all_gather(arrived_labels, "tile", axis=0, tiled=True)
    tile = lax.axis_index("tile")
    swap = [(i, i ^ 1) for i in range(tile_count)]
    half = tile % 2
    partner_rows = lax.ppermute(arrived, "tile", swap)
    pair_rows = jnp.concatenate([arrived, partner_rows], axis=0)
    owners = jnp.where(jnp.arange(2 * CL_DEV) < CL_DEV, tile, tile ^ 1)
    own_ids = (
        lax.axis_index("mass") * per_window
        + owners * CL_DEV
        + jnp.arange(2 * CL_DEV, dtype=jnp.int32) % CL_DEV
    )
    one_hot = (own_ids[:, None] == gathered_labels[None, :]).astype(jnp.bfloat16)
    outs = gram_consensus(half.reshape(1), pair_rows, one_hot, gathered)
    gram_tiles, theirs, sums_mine, sums_theirs = outs[0], outs[1:-2], outs[-2], outs[-1]
    other = (1 - half) * (gathered.shape[0] // 2)
    for p, piece in enumerate(theirs):
        returned = lax.ppermute(piece, "tile", swap)
        gram_tiles = lax.dynamic_update_slice(gram_tiles, returned, (p * piece.shape[0], other))
    gram_tiles, from_partner = lax.optimization_barrier(
        (gram_tiles, lax.ppermute(sums_theirs, "tile", swap))
    )
    consensus = sums_mine + from_partner
    return (gram_tiles, consensus)


def solution(mesh):
    in_specs = (P(("mass", "tile"), None), P(("mass", "tile"), None), P(("mass", "tile")))
    out_specs = (P(("mass", "tile"), None), P(("mass", "tile"), None))
    return jax.shard_map(shards, mesh=mesh, in_specs=in_specs, out_specs=out_specs, check_vma=False)
```

```python
import functools

import jax
import jax.numpy as jnp
from jax import lax
from jax.experimental import pallas as pl
from jax.experimental.pallas import tpu as pltpu
from jax.sharding import PartitionSpec as P

CL_DEV = 4

def _gram_consensus_kernel(scale, rows, pieces, half_ref, a_ref, oh_ref, p_ref, mine_ref, *out_refs):
    theirs_refs, c_mine_ref, c_theirs_ref = out_refs[:pieces], out_refs[pieces], out_refs[pieces + 1]
    j = pl.program_id(0)
    blk = p_ref[...]
    res = lax.dot_general(
        a_ref[...], blk, (((1,), (1,)), ((), ())), preferred_element_type=jnp.float32
    ) * scale
    mine_ref[...] = res[:rows]
    step = rows // pieces
    for p, ref in enumerate(theirs_refs):
        ref[...] = res[rows + p * step:rows + (p + 1) * step]

    @pl.when(j == 0)
    def _():
        c_mine_ref[...] = jnp.zeros_like(c_mine_ref)
        c_theirs_ref[...] = jnp.zeros_like(c_theirs_ref)

    sums = jnp.dot(oh_ref[...], blk, preferred_element_type=jnp.float32)
    heads = sums.shape[0] // 2
    c_mine_ref[...] += sums[:heads]
    c_theirs_ref[...] += sums[heads:]


def gram_consensus(half, pair_rows, one_hot, gathered, pieces=2, block_rows=1024):
    rows = pair_rows.shape[0] // 2
    bins = pair_rows.shape[1]
    total = gathered.shape[0]
    heads = one_hot.shape[0]
    steps = total // 2 // block_rows
    step = rows // pieces
    flops = 2 * 2 * rows * (total // 2) * bins + 2 * heads * (total // 2) * bins
    bytes_accessed = 2 * (2 * rows * bins + heads * total // 2 + total // 2 * bins) + 4 * (
        2 * rows * total // 2 + heads * bins
    )
    grid_spec = pltpu.PrefetchScalarGridSpec(
        num_scalar_prefetch=1,
        grid=(steps,),
        in_specs=[
            pl.BlockSpec((2 * rows, bins), lambda j, h: (0, 0)),
            pl.BlockSpec((heads, block_rows), lambda j, h: (0, h[0] * steps + j)),
            pl.BlockSpec((block_rows, bins), lambda j, h: (h[0] * steps + j, 0)),
        ],
        out_specs=[pl.BlockSpec((rows, block_rows), lambda j, h: (0, h[0] * steps + j))]
        + [pl.BlockSpec((step, block_rows), lambda j, h: (0, j)) for _ in range(pieces)]
        + [pl.BlockSpec((heads // 2, bins), lambda j, h: (0, 0))] * 2,
    )
    return pl.pallas_call(
        functools.partial(_gram_consensus_kernel, 1.0 / bins, rows, pieces),
        grid_spec=grid_spec,
        out_shape=[jax.ShapeDtypeStruct((rows, total), jnp.float32)]
        + [jax.ShapeDtypeStruct((step, total // 2), jnp.float32) for _ in range(pieces)]
        + [jax.ShapeDtypeStruct((heads // 2, bins), jnp.float32)] * 2,
        compiler_params=pltpu.CompilerParams(dimension_semantics=("arbitrary",)),
        cost_estimate=pl.CostEstimate(flops=flops, bytes_accessed=bytes_accessed, transcendentals=0),
    )(half, pair_rows, one_hot, gathered)


def exchange_over_mass(pieces, mass_count):
    me = lax.axis_index("mass")
    ahead = [(i, (i + 1) % mass_count) for i in range(mass_count)]
    behind = [(i, (i - 1) % mass_count) for i in range(mass_count)]
    from_behind = lax.ppermute(pieces[(me + 1) % mass_count], "mass", ahead)
    from_ahead = lax.ppermute(pieces[(me - 1) % mass_count], "mass", behind)
    far = pieces[(me + 2) % mass_count]
    half = far.shape[0] // 2
    first = lax.ppermute(lax.ppermute(far[:half], "mass", ahead), "mass", ahead)
    second = lax.ppermute(lax.ppermute(far[half:], "mass", behind), "mass", behind)
    opposite = jnp.concatenate([first, second], axis=0)
    stacked = jnp.stack([pieces[me], from_behind, opposite, from_ahead])
    return stacked[(me - jnp.arange(mass_count)) % mass_count]


def shards(spectra, window, cluster):
    s_dev, num_bins = spectra.shape
    mass_count = lax.axis_size("mass")
    tile_count = lax.axis_size("tile")
    per_window = CL_DEV * tile_count
    capacity = 2 * s_dev // mass_count
    slot_count = mass_count * capacity
    values = spectra.astype(jnp.float32)
    scaled = (values * lax.rsqrt(jnp.mean(values * values, axis=1, keepdims=True) + 1e-06)).astype(
        jnp.bfloat16
    )
    target = window[:, 0]
    global_ids = target * per_window + cluster
    member = (target[:, None] == jnp.arange(mass_count, dtype=jnp.int32)[None, :]).astype(jnp.int32)
    before = jnp.cumsum(member, axis=0) - member
    slot_rank = jnp.sum(before * member, axis=1)
    position = target * capacity + slot_rank
    chosen = jnp.arange(slot_count, dtype=jnp.int32)[:, None] == position[None, :]
    outgoing = jnp.dot(
        chosen.astype(jnp.bfloat16), scaled, preferred_element_type=jnp.float32
    ).astype(jnp.bfloat16)
    outgoing = outgoing.reshape(mass_count, capacity, num_bins)
    labels = jnp.max(jnp.where(chosen, global_ids[None, :], -1), axis=1).reshape(
        mass_count, capacity
    )
    arrived = exchange_over_mass(outgoing, mass_count)
    arrived_labels = exchange_over_mass(labels, mass_count)
    arrived = arrived.reshape(slot_count, num_bins)
    arrived_labels = arrived_labels.reshape(slot_count)
    gathered = lax.all_gather(arrived, "tile", axis=0, tiled=True)
    gathered_labels = lax.all_gather(arrived_labels, "tile", axis=0, tiled=True)
    tile = lax.axis_index("tile")
    swap = [(i, i ^ 1) for i in range(tile_count)]
    half = tile % 2
    partner_rows = lax.ppermute(arrived, "tile", swap)
    pair_rows = jnp.concatenate([arrived, partner_rows], axis=0)
    owners = jnp.where(jnp.arange(2 * CL_DEV) < CL_DEV, tile, tile ^ 1)
    own_ids = (
        lax.axis_index("mass") * per_window
        + owners * CL_DEV
        + jnp.arange(2 * CL_DEV, dtype=jnp.int32) % CL_DEV
    )
    one_hot = (own_ids[:, None] == gathered_labels[None, :]).astype(jnp.bfloat16)
    outs = gram_consensus(half.reshape(1), pair_rows, one_hot, gathered)
    gram_tiles, theirs, sums_mine, sums_theirs = outs[0], outs[1:-2], outs[-2], outs[-1]
    other = (1 - half) * (gathered.shape[0] // 2)
    for p, piece in enumerate(theirs):
        returned = lax.ppermute(piece, "tile", swap)
        gram_tiles = lax.dynamic_update_slice(gram_tiles, returned, (p * piece.shape[0], other))
    gram_tiles, from_partner = lax.optimization_barrier(
        (gram_tiles, lax.ppermute(sums_theirs, "tile", swap))
    )
    consensus = sums_mine + from_partner
    return (gram_tiles, consensus)


def solution(mesh):
    in_specs = (P(("mass", "tile"), None), P(("mass", "tile"), None), P(("mass", "tile")))
    out_specs = (P(("mass", "tile"), None), P(("mass", "tile"), None))
    return jax.shard_map(shards, mesh=mesh, in_specs=in_specs, out_specs=out_specs, check_vma=False)
```

```python
import functools

import jax
import jax.numpy as jnp
from jax import lax
from jax.experimental import pallas as pl
from jax.experimental.pallas import tpu as pltpu
from jax.sharding import PartitionSpec as P

CL_DEV = 4

def _gram_consensus_kernel(scale, rows, pieces, half_ref, a_ref, oh_ref, p_ref, mine_ref, *out_refs):
    theirs_refs, c_mine_ref, c_theirs_ref = out_refs[:pieces], out_refs[pieces], out_refs[pieces + 1]
    j = pl.program_id(0)
    blk = p_ref[...]
    res = lax.dot_general(
        a_ref[...], blk, (((1,), (1,)), ((), ())), preferred_element_type=jnp.float32
    ) * scale
    mine_ref[...] = res[:rows]
    step = rows // pieces
    for p, ref in enumerate(theirs_refs):
        ref[...] = res[rows + p * step:rows + (p + 1) * step]

    @pl.when(j == 0)
    def _():
        c_mine_ref[...] = jnp.zeros_like(c_mine_ref)
        c_theirs_ref[...] = jnp.zeros_like(c_theirs_ref)

    sums = jnp.dot(oh_ref[...], blk, preferred_element_type=jnp.float32)
    heads = sums.shape[0] // 2
    c_mine_ref[...] += sums[:heads]
    c_theirs_ref[...] += sums[heads:]


def gram_consensus(half, pair_rows, one_hot, gathered, pieces=2, block_rows=512):
    rows = pair_rows.shape[0] // 2
    bins = pair_rows.shape[1]
    total = gathered.shape[0]
    heads = one_hot.shape[0]
    steps = total // 2 // block_rows
    step = rows // pieces
    flops = 2 * 2 * rows * (total // 2) * bins + 2 * heads * (total // 2) * bins
    bytes_accessed = 2 * (2 * rows * bins + heads * total // 2 + total // 2 * bins) + 4 * (
        2 * rows * total // 2 + heads * bins
    )
    grid_spec = pltpu.PrefetchScalarGridSpec(
        num_scalar_prefetch=1,
        grid=(steps,),
        in_specs=[
            pl.BlockSpec((2 * rows, bins), lambda j, h: (0, 0)),
            pl.BlockSpec((heads, block_rows), lambda j, h: (0, h[0] * steps + j)),
            pl.BlockSpec((block_rows, bins), lambda j, h: (h[0] * steps + j, 0)),
        ],
        out_specs=[pl.BlockSpec((rows, block_rows), lambda j, h: (0, h[0] * steps + j))]
        + [pl.BlockSpec((step, block_rows), lambda j, h: (0, j)) for _ in range(pieces)]
        + [pl.BlockSpec((heads // 2, bins), lambda j, h: (0, 0))] * 2,
    )
    return pl.pallas_call(
        functools.partial(_gram_consensus_kernel, 1.0 / bins, rows, pieces),
        grid_spec=grid_spec,
        out_shape=[jax.ShapeDtypeStruct((rows, total), jnp.float32)]
        + [jax.ShapeDtypeStruct((step, total // 2), jnp.float32) for _ in range(pieces)]
        + [jax.ShapeDtypeStruct((heads // 2, bins), jnp.float32)] * 2,
        compiler_params=pltpu.CompilerParams(dimension_semantics=("arbitrary",)),
        cost_estimate=pl.CostEstimate(flops=flops, bytes_accessed=bytes_accessed, transcendentals=0),
    )(half, pair_rows, one_hot, gathered)


def exchange_over_mass(pieces, mass_count):
    me = lax.axis_index("mass")
    ahead = [(i, (i + 1) % mass_count) for i in range(mass_count)]
    behind = [(i, (i - 1) % mass_count) for i in range(mass_count)]
    from_behind = lax.ppermute(pieces[(me + 1) % mass_count], "mass", ahead)
    from_ahead = lax.ppermute(pieces[(me - 1) % mass_count], "mass", behind)
    far = pieces[(me + 2) % mass_count]
    half = far.shape[0] // 2
    first = lax.ppermute(lax.ppermute(far[:half], "mass", ahead), "mass", ahead)
    second = lax.ppermute(lax.ppermute(far[half:], "mass", behind), "mass", behind)
    opposite = jnp.concatenate([first, second], axis=0)
    stacked = jnp.stack([pieces[me], from_behind, opposite, from_ahead])
    return stacked[(me - jnp.arange(mass_count)) % mass_count]


def shards(spectra, window, cluster):
    s_dev, num_bins = spectra.shape
    mass_count = lax.axis_size("mass")
    tile_count = lax.axis_size("tile")
    per_window = CL_DEV * tile_count
    capacity = 2 * s_dev // mass_count
    slot_count = mass_count * capacity
    values = spectra.astype(jnp.float32)
    scaled = (values * lax.rsqrt(jnp.mean(values * values, axis=1, keepdims=True) + 1e-06)).astype(
        jnp.bfloat16
    )
    target = window[:, 0]
    global_ids = target * per_window + cluster
    member = (target[:, None] == jnp.arange(mass_count, dtype=jnp.int32)[None, :]).astype(jnp.int32)
    before = jnp.cumsum(member, axis=0) - member
    slot_rank = jnp.sum(before * member, axis=1)
    position = target * capacity + slot_rank
    chosen = jnp.arange(slot_count, dtype=jnp.int32)[:, None] == position[None, :]
    outgoing = jnp.dot(
        chosen.astype(jnp.bfloat16), scaled, preferred_element_type=jnp.float32
    ).astype(jnp.bfloat16)
    outgoing = outgoing.reshape(mass_count, capacity, num_bins)
    labels = jnp.max(jnp.where(chosen, global_ids[None, :], -1), axis=1).reshape(
        mass_count, capacity
    )
    arrived = exchange_over_mass(outgoing, mass_count)
    arrived_labels = exchange_over_mass(labels, mass_count)
    arrived = arrived.reshape(slot_count, num_bins)
    arrived_labels = arrived_labels.reshape(slot_count)
    gathered = lax.all_gather(arrived, "tile", axis=0, tiled=True)
    gathered_labels = lax.all_gather(arrived_labels, "tile", axis=0, tiled=True)
    tile = lax.axis_index("tile")
    swap = [(i, i ^ 1) for i in range(tile_count)]
    half = tile % 2
    partner_rows = lax.ppermute(arrived, "tile", swap)
    pair_rows = jnp.concatenate([arrived, partner_rows], axis=0)
    owners = jnp.where(jnp.arange(2 * CL_DEV) < CL_DEV, tile, tile ^ 1)
    own_ids = (
        lax.axis_index("mass") * per_window
        + owners * CL_DEV
        + jnp.arange(2 * CL_DEV, dtype=jnp.int32) % CL_DEV
    )
    one_hot = (own_ids[:, None] == gathered_labels[None, :]).astype(jnp.bfloat16)
    outs = gram_consensus(half.reshape(1), pair_rows, one_hot, gathered)
    gram_tiles, theirs, sums_mine, sums_theirs = outs[0], outs[1:-2], outs[-2], outs[-1]
    other = (1 - half) * (gathered.shape[0] // 2)
    for p, piece in enumerate(theirs):
        returned = lax.ppermute(piece, "tile", swap)
        gram_tiles = lax.dynamic_update_slice(gram_tiles, returned, (p * piece.shape[0], other))
    gram_tiles, from_partner = lax.optimization_barrier(
        (gram_tiles, lax.ppermute(sums_theirs, "tile", swap))
    )
    consensus = sums_mine + from_partner
    return (gram_tiles, consensus)


def solution(mesh):
    in_specs = (P(("mass", "tile"), None), P(("mass", "tile"), None), P(("mass", "tile")))
    out_specs = (P(("mass", "tile"), None), P(("mass", "tile"), None))
    return jax.shard_map(shards, mesh=mesh, in_specs=in_specs, out_specs=out_specs, check_vma=False)
```

```python
import functools

import jax
import jax.numpy as jnp
from jax import lax
from jax.experimental import pallas as pl
from jax.experimental.pallas import tpu as pltpu
from jax.sharding import PartitionSpec as P

CL_DEV = 4

def _gram_consensus_kernel(scale, rows, pieces, half_ref, a_ref, oh_ref, p_ref, mine_ref, *out_refs):
    theirs_refs, c_mine_ref, c_theirs_ref = out_refs[:pieces], out_refs[pieces], out_refs[pieces + 1]
    j = pl.program_id(0)
    blk = p_ref[...]
    res = lax.dot_general(
        a_ref[...], blk, (((1,), (1,)), ((), ())), preferred_element_type=jnp.float32
    ) * scale
    mine_ref[...] = res[:rows]
    step = rows // pieces
    for p, ref in enumerate(theirs_refs):
        ref[...] = res[rows + p * step:rows + (p + 1) * step]

    @pl.when(j == 0)
    def _():
        c_mine_ref[...] = jnp.zeros_like(c_mine_ref)
        c_theirs_ref[...] = jnp.zeros_like(c_theirs_ref)

    sums = jnp.dot(oh_ref[...], blk, preferred_element_type=jnp.float32)
    heads = sums.shape[0] // 2
    c_mine_ref[...] += sums[:heads]
    c_theirs_ref[...] += sums[heads:]


def gram_consensus(half, pair_rows, one_hot, gathered, pieces=3, block_rows=1024):
    rows = pair_rows.shape[0] // 2
    bins = pair_rows.shape[1]
    total = gathered.shape[0]
    heads = one_hot.shape[0]
    steps = total // 2 // block_rows
    step = rows // pieces
    flops = 2 * 2 * rows * (total // 2) * bins + 2 * heads * (total // 2) * bins
    bytes_accessed = 2 * (2 * rows * bins + heads * total // 2 + total // 2 * bins) + 4 * (
        2 * rows * total // 2 + heads * bins
    )
    grid_spec = pltpu.PrefetchScalarGridSpec(
        num_scalar_prefetch=1,
        grid=(steps,),
        in_specs=[
            pl.BlockSpec((2 * rows, bins), lambda j, h: (0, 0)),
            pl.BlockSpec((heads, block_rows), lambda j, h: (0, h[0] * steps + j)),
            pl.BlockSpec((block_rows, bins), lambda j, h: (h[0] * steps + j, 0)),
        ],
        out_specs=[pl.BlockSpec((rows, block_rows), lambda j, h: (0, h[0] * steps + j))]
        + [pl.BlockSpec((step, block_rows), lambda j, h: (0, j)) for _ in range(pieces)]
        + [pl.BlockSpec((heads // 2, bins), lambda j, h: (0, 0))] * 2,
    )
    return pl.pallas_call(
        functools.partial(_gram_consensus_kernel, 1.0 / bins, rows, pieces),
        grid_spec=grid_spec,
        out_shape=[jax.ShapeDtypeStruct((rows, total), jnp.float32)]
        + [jax.ShapeDtypeStruct((step, total // 2), jnp.float32) for _ in range(pieces)]
        + [jax.ShapeDtypeStruct((heads // 2, bins), jnp.float32)] * 2,
        compiler_params=pltpu.CompilerParams(dimension_semantics=("arbitrary",)),
        cost_estimate=pl.CostEstimate(flops=flops, bytes_accessed=bytes_accessed, transcendentals=0),
    )(half, pair_rows, one_hot, gathered)


def exchange_over_mass(pieces, mass_count):
    me = lax.axis_index("mass")
    ahead = [(i, (i + 1) % mass_count) for i in range(mass_count)]
    behind = [(i, (i - 1) % mass_count) for i in range(mass_count)]
    from_behind = lax.ppermute(pieces[(me + 1) % mass_count], "mass", ahead)
    from_ahead = lax.ppermute(pieces[(me - 1) % mass_count], "mass", behind)
    far = pieces[(me + 2) % mass_count]
    half = far.shape[0] // 2
    first = lax.ppermute(lax.ppermute(far[:half], "mass", ahead), "mass", ahead)
    second = lax.ppermute(lax.ppermute(far[half:], "mass", behind), "mass", behind)
    opposite = jnp.concatenate([first, second], axis=0)
    stacked = jnp.stack([pieces[me], from_behind, opposite, from_ahead])
    return stacked[(me - jnp.arange(mass_count)) % mass_count]


def shards(spectra, window, cluster):
    s_dev, num_bins = spectra.shape
    mass_count = lax.axis_size("mass")
    tile_count = lax.axis_size("tile")
    per_window = CL_DEV * tile_count
    capacity = 2 * s_dev // mass_count
    slot_count = mass_count * capacity
    values = spectra.astype(jnp.float32)
    scaled = (values * lax.rsqrt(jnp.mean(values * values, axis=1, keepdims=True) + 1e-06)).astype(
        jnp.bfloat16
    )
    target = window[:, 0]
    global_ids = target * per_window + cluster
    member = (target[:, None] == jnp.arange(mass_count, dtype=jnp.int32)[None, :]).astype(jnp.int32)
    before = jnp.cumsum(member, axis=0) - member
    slot_rank = jnp.sum(before * member, axis=1)
    position = target * capacity + slot_rank
    chosen = jnp.arange(slot_count, dtype=jnp.int32)[:, None] == position[None, :]
    outgoing = jnp.dot(
        chosen.astype(jnp.bfloat16), scaled, preferred_element_type=jnp.float32
    ).astype(jnp.bfloat16)
    outgoing = outgoing.reshape(mass_count, capacity, num_bins)
    labels = jnp.max(jnp.where(chosen, global_ids[None, :], -1), axis=1).reshape(
        mass_count, capacity
    )
    arrived = exchange_over_mass(outgoing, mass_count)
    arrived_labels = exchange_over_mass(labels, mass_count)
    arrived = arrived.reshape(slot_count, num_bins)
    arrived_labels = arrived_labels.reshape(slot_count)
    gathered = lax.all_gather(arrived, "tile", axis=0, tiled=True)
    gathered_labels = lax.all_gather(arrived_labels, "tile", axis=0, tiled=True)
    tile = lax.axis_index("tile")
    swap = [(i, i ^ 1) for i in range(tile_count)]
    half = tile % 2
    partner_rows = lax.ppermute(arrived, "tile", swap)
    pair_rows = jnp.concatenate([arrived, partner_rows], axis=0)
    owners = jnp.where(jnp.arange(2 * CL_DEV) < CL_DEV, tile, tile ^ 1)
    own_ids = (
        lax.axis_index("mass") * per_window
        + owners * CL_DEV
        + jnp.arange(2 * CL_DEV, dtype=jnp.int32) % CL_DEV
    )
    one_hot = (own_ids[:, None] == gathered_labels[None, :]).astype(jnp.bfloat16)
    outs = gram_consensus(half.reshape(1), pair_rows, one_hot, gathered)
    gram_tiles, theirs, sums_mine, sums_theirs = outs[0], outs[1:-2], outs[-2], outs[-1]
    other = (1 - half) * (gathered.shape[0] // 2)
    for p, piece in enumerate(theirs):
        returned = lax.ppermute(piece, "tile", swap)
        gram_tiles = lax.dynamic_update_slice(gram_tiles, returned, (p * piece.shape[0], other))
    gram_tiles, from_partner = lax.optimization_barrier(
        (gram_tiles, lax.ppermute(sums_theirs, "tile", swap))
    )
    consensus = sums_mine + from_partner
    return (gram_tiles, consensus)


def solution(mesh):
    in_specs = (P(("mass", "tile"), None), P(("mass", "tile"), None), P(("mass", "tile")))
    out_specs = (P(("mass", "tile"), None), P(("mass", "tile"), None))
    return jax.shard_map(shards, mesh=mesh, in_specs=in_specs, out_specs=out_specs, check_vma=False)
```
